128 devices in a mesh: node: 8 (over z, core), local: 16 (over x, y).
Axes of the slice: x: 4, y: 4, z: 4, core: 2. Of those that a mesh axis runs over, the one named last changes fastest.
Arguments:
- tokens: bfloat16 [16384, 4096], P(('node', 'local')), may hold values from -6 to 6
- cotangent: bfloat16 [16384, 4096], P(('node', 'local')), may hold values from -6 to 6
- gate_probs: float32 [16384, 8], P(('node', 'local')), may hold values from 0.02 to 0.5
- experts: int32 [16384, 8], P(('node', 'local')), may hold values from 0 to 127, all different within a row; in each aligned block of 128 rows (0 to 127, 128 to 255, ...) at most 10 rows name the same one
- stratum: int32 [128], P(('node', 'local')), may hold values from 0 to 7
- token_level: int32 [16384], P(('node', 'local')), may hold values from 0 to 63
- w_gate_up: bfloat16 [128, 4096, 1024], P(('node', 'local')), may hold values from -0.09375 to 0.09375
- w_down: bfloat16 [128, 512, 4096], P(('node', 'local')), may hold values from -0.25 to 0.25
Outputs:
- grad_tokens: bfloat16 [16384, 4096], P(('node', 'local'))
- grad_probs: bfloat16 [16384, 8], P(('node', 'local'))
The draws below stay inside these ranges and needn't reach their ends.
Inputs may be any that keep to these rules, and one draw needn't show every extreme that they name: Among the tokens of one device no expert is named more than 10 times; in every draw some expert is named exactly 10 times by the tokens of some device. A token names 8 different experts.
All inputs are finite; a program needn't handle non-finite values.
Results may differ from the reference program's by a relative error of at most 0.013.
Values may be sent and summed in bfloat16 or wider, within the bound.
No kernel may reach another device: no remote copies, remote signals or barrier semaphores. Data moves between devices by JAX's collectives and lax.ppermute only.
A program may use at most 192 MiB of HBM per device.

```python
import math
import jax
import jax.numpy as jnp
import numpy as np
from jax import lax

D = 4096
H = 512
TOP = 8
STRATA = 8
LEVELS = 64
TOK_DEV = 128
EXPERTS = 128
TOKENS = 16384
CAP = 10
N_NODE = 8
N_LOCAL = 16


def with_ends(entries, key, smallest, largest):
    extent = entries.shape
    place = [jax.random.randint(jax.random.fold_in(key, axis), (), 0, extent[axis]) for axis in range(len(extent))]
    entries = entries.at[tuple(place)].set(smallest)
    longest = extent.index(max(extent))
    place[longest] = (place[longest] + 1) % extent[longest]
    return entries.at[tuple(place)].set(largest)


def block_scale(rng, dims, split, smallest, top_value):
    level = 1.0
    for dim, blocks in split:
        draws = jax.random.uniform(jax.random.fold_in(jax.random.fold_in(rng, 6), dim), (blocks,), jnp.float32, smallest / len(split), top_value / len(split))
        level = level * jnp.repeat(jnp.exp(draws), dims[dim] // blocks).reshape((-1,) + (1,) * (len(dims) - 1 - dim))
    return level


def assign_block(stream_key, own, number, rows, number_of, top, most, lean):
    sequence = jax.random.permutation(stream_key, number_of)
    crowded, usual = shares(number_of, rows * top, most, lean, True), shares(number_of, rows * top, most, lean, False)
    places = jnp.arange(number_of)

    def named(lengths, rotation):
        used = int((lengths > 0).sum())
        fixed = max(1, used // 4)
        passed = fixed + (places - fixed + rotation * (used - fixed)) % max(1, number_of - fixed)
        return jnp.zeros((number_of,), jnp.int32).at[sequence[jnp.where(places < fixed, places, passed)]].set(jnp.asarray(lengths, jnp.int32))

    lengths = jnp.where(number % 4 == 0, named(crowded, number // 4), named(usual, number - number // 4 - 1))
    mixed = jax.random.permutation(jax.random.fold_in(own, 3), number_of)
    giver, receiver = mixed[0:number_of // 2 * 2:2], mixed[1:number_of // 2 * 2:2]
    margin = jnp.minimum(lengths[giver] - 1, most - lengths[receiver]) // 2
    margin = jnp.where((giver == sequence[0]) | (receiver == sequence[0]) | (lengths[receiver] == 0), 0, jnp.maximum(margin, 0))
    passed = jax.random.randint(jax.random.fold_in(own, 4), (number_of // 2,), 0, 1 << 20) % (margin + 1)
    lengths = lengths.at[giver].add(-passed).at[receiver].add(passed)
    members = jnp.searchsorted(jnp.cumsum(lengths), jnp.arange(rows * top), side="right").astype(jnp.int32)
    table = members.reshape(top, rows).T
    table = table[jax.random.permutation(jax.random.fold_in(own, 1), rows)]
    rotation = jax.random.randint(jax.random.fold_in(own, 2), (rows, 1), 0, top)
    return jnp.take_along_axis(table, (jnp.arange(top)[None, :] + rotation) % top, axis=1)


def shares(amount, total, reach, lean, full):
    weights = [(1 << 20) // math.isqrt(rank ** lean) + 1 for rank in range(1, amount + 1)]
    largest = reach if full else min(reach, max(-(-total // amount), total * weights[0] // sum(weights)))
    least = 1 if total - largest >= amount - 1 else 0
    given, spare = [largest] + [least] * (amount - 1), total - largest - least * (amount - 1)
    while spare > 0:
        candidates = [i for i in range(1, amount) if given[i] < largest] or [i for i in range(1, amount) if given[i] < reach]
        whole, remaining = sum([weights[i] for i in candidates]), spare
        for i in candidates:
            extra = min(reach - given[i], max(1, remaining * weights[i] // whole), spare)
            given[i] = given[i] + extra
            spare = spare - extra
    return np.array(given)


def scatter_about(stream_key, extent, spread, most, cuts=(), held_as=jnp.bfloat16):
    entries = jax.random.normal(stream_key, extent, jnp.float32) * spread
    if len(cuts) > 0:
        entries = block_scale(stream_key, extent, cuts, -0.22, 0.18) * entries
    return jnp.clip(entries, min=-most, max=most).astype(held_as)


def setup_inputs(seed: int = 0) -> dict:
    keys = jax.random.split(jax.random.key(seed), 9)
    tokens = scatter_about(keys[0], (TOKENS, D), 1.0, 6.0, ((0, 128),))
    cotangent = scatter_about(keys[1], (TOKENS, D), 1.0, 6.0, ((0, 128),))
    gate_probs = jnp.clip(jnp.exp(math.log(0.5) - 3.218876 * jax.random.uniform(keys[2], (TOKENS, TOP), jnp.float32) ** block_scale(keys[2], (TOKENS, TOP), ((0, 128),), -0.2, 0.2)), 0.02, 0.5)
    experts_keys = jax.random.split(jax.random.fold_in(keys[3], 1), TOKENS // TOK_DEV)
    experts_turns = jax.random.permutation(jax.random.fold_in(keys[3], 3), TOKENS // TOK_DEV)
    experts = jax.vmap(lambda own, number: assign_block(jax.random.fold_in(keys[3], 2), own, number, TOK_DEV, EXPERTS, TOP, CAP, 2))(experts_keys, experts_turns).reshape((TOKENS, TOP))
    stratum = with_ends(jax.random.randint(keys[4], (N_NODE * N_LOCAL,), 0, STRATA), jax.random.fold_in(keys[4], 1), 0, STRATA - 1).astype(jnp.int32)
    token_level = with_ends(jax.random.randint(keys[5], (TOKENS,), 0, LEVELS), jax.random.fold_in(keys[5], 1), 0, LEVELS - 1).astype(jnp.int32)
    w_gate_up = scatter_about(keys[6], (EXPERTS, D, 2 * H), D ** -0.5, 0.09375, ((0, 128),))
    w_down = scatter_about(keys[7], (EXPERTS, H, D), H ** -0.5, 0.25, ((0, 128),))
    return {"tokens": tokens, "cotangent": cotangent, "gate_probs": gate_probs, "experts": experts, "stratum": stratum, "token_level": token_level, "w_gate_up": w_gate_up, "w_down": w_down}


def expert_grads(inputs, upstream, weight_in, weight_out):
    hidden_units = weight_out.shape[0]
    projected = jnp.dot(inputs, weight_in, preferred_element_type=jnp.float32)
    gate_part = projected[:, :hidden_units]
    up_part = projected[:, hidden_units:]
    sigmoid_gate = jax.nn.sigmoid(gate_part)
    activated = gate_part * sigmoid_gate
    hidden = (activated * up_part).astype(jnp.bfloat16)
    backward = jnp.dot(upstream, weight_out.T, preferred_element_type=jnp.float32)
    prob_grad = jnp.sum(hidden.astype(jnp.float32) * backward, axis=1).astype(jnp.bfloat16)
    grad_gate = backward * up_part * sigmoid_gate * (1.0 + gate_part * (1.0 - sigmoid_gate))
    grad_up = backward * activated
    stacked = jnp.concatenate([grad_gate, grad_up], axis=1).astype(jnp.bfloat16)
    row_grads = jnp.dot(stacked, weight_in.T, preferred_element_type=jnp.float32).astype(jnp.bfloat16)
    return row_grads, prob_grad


def reference(tokens, cotangent, gate_probs, experts, stratum, token_level, w_gate_up, w_down):
    device_count = N_NODE * N_LOCAL
    slot_count = device_count * CAP
    owner_device = jnp.arange(TOKENS, dtype=jnp.int32) // TOK_DEV
    token_stratum = stratum[owner_device]
    masked = token_level * STRATA < (token_stratum + 1) * LEVELS
    loss_weight = jnp.where(masked, STRATA / (token_stratum + 1).astype(jnp.float32), jnp.float32(0.0))
    upstream = (cotangent.astype(jnp.float32) * loss_weight[:, None]).astype(jnp.bfloat16)
    chosen = experts.reshape(-1)
    pair_count = chosen.shape[0]
    onehot = (chosen[:, None] == jnp.arange(EXPERTS, dtype=jnp.int32)[None, :]).astype(jnp.int32)
    ranking = jnp.sum((jnp.cumsum(onehot, axis=0) - 1) * onehot, axis=1)
    placed = chosen * slot_count + ranking
    owner_table = jnp.full((EXPERTS * slot_count,), pair_count, jnp.int32)
    owner_table = owner_table.at[placed].set(jnp.arange(pair_count, dtype=jnp.int32)).reshape(EXPERTS, slot_count)
    padded_tokens = jnp.concatenate([tokens, jnp.zeros((1, D), jnp.bfloat16)], axis=0)
    padded_upstream = jnp.concatenate([upstream, jnp.zeros((1, D), jnp.bfloat16)], axis=0)
    padded_probs = jnp.concatenate([gate_probs.reshape(-1), jnp.zeros((1,), jnp.float32)], axis=0)

    def per_expert(carry, pieces):
        grad_accum, prob_accum = carry
        weight_in, weight_out, pair_index = pieces
        token_index = pair_index // TOP
        row_grads, prob_grad = expert_grads(padded_tokens[token_index], padded_upstream[token_index], weight_in, weight_out)
        scaled = padded_probs[pair_index][:, None] * row_grads.astype(jnp.float32)
        grad_accum = grad_accum.at[token_index].add(scaled, mode="drop")
        prob_accum = prob_accum.at[pair_index].set(prob_grad, mode="drop")
        return (grad_accum, prob_accum), None

    start = (jnp.zeros((TOKENS, D), jnp.float32), jnp.zeros((pair_count,), jnp.bfloat16))
    (grad_accum, prob_accum), unused = lax.scan(per_expert, start, (w_gate_up, w_down, owner_table))
    return grad_accum.astype(jnp.bfloat16), prob_accum.reshape(TOKENS, TOP)
```

```python
import jax
import jax.numpy as jnp
from jax import lax
from jax.sharding import PartitionSpec as P

STRATA = 8
LEVELS = 64


def expert_grads(inputs, upstream, weight_in, weight_out):
    hidden_units = weight_out.shape[0]
    projected = jnp.dot(inputs, weight_in, preferred_element_type=jnp.float32)
    gate_part = projected[:, :hidden_units]
    up_part = projected[:, hidden_units:]
    sigmoid_gate = jax.nn.sigmoid(gate_part)
    activated = gate_part * sigmoid_gate
    hidden = (activated * up_part).astype(jnp.bfloat16)
    backward = jnp.dot(upstream, weight_out.T, preferred_element_type=jnp.float32)
    prob_grad = jnp.sum(hidden.astype(jnp.float32) * backward, axis=1).astype(jnp.bfloat16)
    grad_gate = backward * up_part * sigmoid_gate * (1.0 + gate_part * (1.0 - sigmoid_gate))
    grad_up = backward * activated
    stacked = jnp.concatenate([grad_gate, grad_up], axis=1).astype(jnp.bfloat16)
    row_grads = jnp.dot(stacked, weight_in.T, preferred_element_type=jnp.float32).astype(
        jnp.bfloat16
    )
    return (row_grads, prob_grad)


def body(tokens, cotangent, gate_probs, experts, stratum, token_level, w_gate_up, w_down):
    device_count = lax.axis_size(("node", "local"))
    token_rows, chosen_count = experts.shape
    width = tokens.shape[1]
    capacity = max(2, token_rows * chosen_count * 5 // (4 * device_count))
    stratum_here = stratum[0]
    masked = token_level * STRATA < (stratum_here + 1) * LEVELS
    loss_weight = jnp.where(
        masked, STRATA / (stratum_here + 1).astype(jnp.float32), jnp.float32(0.0)
    )
    upstream = (cotangent.astype(jnp.float32) * loss_weight[:, None]).astype(jnp.bfloat16)
    chosen = experts.reshape(-1)
    pair_count = chosen.shape[0]
    onehot = (chosen[:, None] == jnp.arange(device_count, dtype=jnp.int32)[None, :]).astype(
        jnp.int32
    )
    ranking = jnp.sum((jnp.cumsum(onehot, axis=0) - 1) * onehot, axis=1)
    placed = chosen * capacity + ranking
    owner_table = jnp.full((device_count * capacity,), pair_count, jnp.int32)
    owner_table = owner_table.at[placed].set(jnp.arange(pair_count, dtype=jnp.int32))
    token_index = owner_table // chosen_count
    padded_tokens = jnp.concatenate([tokens, jnp.zeros((1, width), jnp.bfloat16)], axis=0)
    padded_upstream = jnp.concatenate([upstream, jnp.zeros((1, width), jnp.bfloat16)], axis=0)
    block_rows = 16 if (capacity * width) % (16 * 128) == 0 else capacity
    block = (device_count, block_rows, capacity * width // block_rows)
    send_tokens = padded_tokens[token_index].reshape(block)
    send_upstream = padded_upstream[token_index].reshape(block)
    weight_in = w_gate_up[0]
    weight_out = w_down[0]
    arrived_tokens = lax.all_to_all(
        send_tokens, ("node", "local"), split_axis=0, concat_axis=0, tiled=True
    )
    sources = arrived_tokens.shape[0]
    items = capacity
    row_grads, prob_grad = expert_grads(
        arrived_tokens.reshape(sources * items, width),
        lax.all_to_all(
            send_upstream, ("node", "local"), split_axis=0, concat_axis=0, tiled=True
        ).reshape(sources * items, width),
        weight_in,
        weight_out,
    )
    row_grads, prob_grad = (
        row_grads.reshape(block),
        prob_grad.reshape(sources, items),
    )
    home_grads = lax.all_to_all(
        row_grads, ("node", "local"), split_axis=0, concat_axis=0, tiled=True
    )
    home_probs = lax.all_to_all(
        prob_grad, ("node", "local"), split_axis=0, concat_axis=0, tiled=True
    )
    pair_grads = home_grads.reshape(device_count * capacity, width)[placed]
    weighted = (
        pair_grads.astype(jnp.float32).reshape(token_rows, chosen_count, width)
        * gate_probs[:, :, None]
    )
    grad_tokens = jnp.sum(weighted, axis=1).astype(jnp.bfloat16)
    grad_probs = home_probs.reshape(-1)[placed].reshape(token_rows, chosen_count)
    return (grad_tokens, grad_probs)


def solution(mesh):
    placed = (
        P(("node", "local"), None),
        P(("node", "local"), None),
        P(("node", "local"), None),
        P(("node", "local"), None),
        P(("node", "local")),
        P(("node", "local")),
        P(("node", "local"), None, None),
        P(("node", "local"), None, None),
    )
    return jax.shard_map(
        body,
        mesh=mesh,
        in_specs=placed,
        out_specs=(P(("node", "local"), None), P(("node", "local"), None)),
        check_vma=False,
    )
```

```python
import jax
import jax.numpy as jnp
from jax import lax
from jax.sharding import PartitionSpec as P

STRATA = 8
LEVELS = 64


def expert_grads(inputs, upstream, weight_in, weight_out):
    hidden_units = weight_out.shape[0]
    projected = jnp.dot(inputs, weight_in, preferred_element_type=jnp.float32)
    gate_part = projected[:, :hidden_units]
    up_part = projected[:, hidden_units:]
    sigmoid_gate = jax.nn.sigmoid(gate_part)
    activated = gate_part * sigmoid_gate
    hidden = (activated * up_part).astype(jnp.bfloat16)
    backward = jnp.dot(upstream, weight_out.T, preferred_element_type=jnp.float32)
    prob_grad = jnp.sum(hidden.astype(jnp.float32) * backward, axis=1).astype(jnp.bfloat16)
    grad_gate = backward * up_part * sigmoid_gate * (1.0 + gate_part * (1.0 - sigmoid_gate))
    grad_up = backward * activated
    stacked = jnp.concatenate([grad_gate, grad_up], axis=1).astype(jnp.bfloat16)
    row_grads = jnp.dot(stacked, weight_in.T, preferred_element_type=jnp.float32).astype(
        jnp.bfloat16
    )
    return (row_grads, prob_grad)


def body(tokens, cotangent, gate_probs, experts, stratum, token_level, w_gate_up, w_down):
    axes = ("node", "local")
    device_count = lax.axis_size(axes)
    token_rows, chosen_count = experts.shape
    width = tokens.shape[1]
    capacity = max(2, token_rows * chosen_count * 5 // (4 * device_count))
    stratum_here = stratum[0]
    masked = token_level * STRATA < (stratum_here + 1) * LEVELS
    loss_weight = jnp.where(
        masked, STRATA / (stratum_here + 1).astype(jnp.float32), jnp.float32(0.0)
    )
    upstream = (cotangent.astype(jnp.float32) * loss_weight[:, None]).astype(jnp.bfloat16)
    chosen = experts.reshape(-1)
    pair_count = chosen.shape[0]
    onehot = (chosen[:, None] == jnp.arange(device_count, dtype=jnp.int32)[None, :]).astype(
        jnp.int32
    )
    ranking = jnp.sum((jnp.cumsum(onehot, axis=0) - 1) * onehot, axis=1)
    placed = chosen * capacity + ranking
    owner_table = jnp.full((device_count * capacity,), pair_count, jnp.int32)
    owner_table = owner_table.at[placed].set(jnp.arange(pair_count, dtype=jnp.int32))
    token_index = (owner_table // chosen_count).reshape(device_count, capacity)
    padded_tokens = jnp.concatenate([tokens, jnp.zeros((1, width), jnp.bfloat16)], axis=0)
    padded_upstream = jnp.concatenate([upstream, jnp.zeros((1, width), jnp.bfloat16)], axis=0)
    weight_in = w_gate_up[0]
    weight_out = w_down[0]
    chunks = 2 if capacity % 2 == 0 else 1
    per_chunk = capacity // chunks
    block_rows = 16 if (per_chunk * width) % (16 * 128) == 0 else per_chunk
    block = (device_count, block_rows, per_chunk * width // block_rows)
    chunk_slots = device_count * per_chunk
    def exchange(part):
        return lax.all_to_all(part, axes, 0, 0, tiled=True)

    def send_of(c):
        index = token_index[:, c * per_chunk : (c + 1) * per_chunk].reshape(-1)
        return jnp.concatenate(
            [padded_tokens[index].reshape(block), padded_upstream[index].reshape(block)], axis=1
        )

    def compute(arrived):
        row_grads, prob_grad = expert_grads(
            arrived[:, :block_rows].reshape(chunk_slots, width),
            arrived[:, block_rows:].reshape(chunk_slots, width),
            weight_in,
            weight_out,
        )
        return row_grads.reshape(block), prob_grad.reshape(device_count, 1, per_chunk)

    def combine(c, home):
        local = ranking - c * per_chunk
        inside = (local >= 0) & (local < per_chunk)
        slot = jnp.where(inside, chosen * per_chunk + local, -1).reshape(token_rows, chosen_count)
        weight = jnp.where(inside.reshape(token_rows, chosen_count), gate_probs, 0.0)
        table = jnp.sum(
            jnp.where(
                slot[:, :, None] == jnp.arange(chunk_slots, dtype=jnp.int32)[None, None, :],
                weight[:, :, None],
                0.0,
            ),
            axis=1,
        )
        high = table.astype(jnp.bfloat16)
        low = (table - high.astype(jnp.float32)).astype(jnp.bfloat16)
        home = home.reshape(chunk_slots, width)
        return jnp.dot(high, home, preferred_element_type=jnp.float32) + jnp.dot(
            low, home, preferred_element_type=jnp.float32
        )

    arrived = exchange(send_of(0))
    grad_tokens = None
    prob_parts = []
    pending = None
    for c in range(chunks):
        row_grads, prob_grad = compute(arrived)
        if c + 1 < chunks:
            arrived = exchange(send_of(c + 1))
            arrived, row_grads, prob_grad = lax.optimization_barrier(
                (arrived, row_grads, prob_grad)
            )
        if pending is not None:
            pending, row_grads, prob_grad = lax.optimization_barrier(
                (pending, row_grads, prob_grad)
            )
            part = combine(c - 1, pending[0])
            prob_parts.append(pending[1].reshape(device_count, per_chunk))
            grad_tokens = part if grad_tokens is None else grad_tokens + part
        pending = (exchange(row_grads), exchange(prob_grad))
    part = combine(chunks - 1, pending[0])
    prob_parts.append(pending[1].reshape(device_count, per_chunk))
    grad_tokens = part if grad_tokens is None else grad_tokens + part
    home_probs = jnp.concatenate(prob_parts, axis=1).reshape(-1)
    grad_probs = home_probs[placed].reshape(token_rows, chosen_count)
    return (grad_tokens.astype(jnp.bfloat16), grad_probs)


def solution(mesh):
    placed = (
        P(("node", "local"), None),
        P(("node", "local"), None),
        P(("node", "local"), None),
        P(("node", "local"), None),
        P(("node", "local")),
        P(("node", "local")),
        P(("node", "local"), None, None),
        P(("node", "local"), None, None),
    )
    return jax.shard_map(
        body,
        mesh=mesh,
        in_specs=placed,
        out_specs=(P(("node", "local"), None), P(("node", "local"), None)),
        check_vma=False,
    )
```

```python
import jax
import jax.numpy as jnp
from jax import lax
from jax.sharding import PartitionSpec as P

STRATA = 8
LEVELS = 64
CHUNK_SIZES = (5, 5)


def expert_grads(inputs, upstream, weight_in, weight_out):
    hidden_units = weight_out.shape[0]
    projected = jnp.dot(inputs, weight_in, preferred_element_type=jnp.float32)
    gate_part = projected[:, :hidden_units]
    up_part = projected[:, hidden_units:]
    sigmoid_gate = jax.nn.sigmoid(gate_part)
    activated = gate_part * sigmoid_gate
    hidden = (activated * up_part).astype(jnp.bfloat16)
    backward = jnp.dot(upstream, weight_out.T, preferred_element_type=jnp.float32)
    prob_grad = jnp.sum(hidden.astype(jnp.float32) * backward, axis=1).astype(jnp.bfloat16)
    grad_gate = backward * up_part * sigmoid_gate * (1.0 + gate_part * (1.0 - sigmoid_gate))
    grad_up = backward * activated
    stacked = jnp.concatenate([grad_gate, grad_up], axis=1).astype(jnp.bfloat16)
    row_grads = jnp.dot(stacked, weight_in.T, preferred_element_type=jnp.float32).astype(
        jnp.bfloat16
    )
    return (row_grads, prob_grad)


def body(tokens, cotangent, gate_probs, experts, stratum, token_level, w_gate_up, w_down):
    axes = ("node", "local")
    device_count = lax.axis_size(axes)
    token_rows, chosen_count = experts.shape
    width = tokens.shape[1]
    capacity = max(2, token_rows * chosen_count * 5 // (4 * device_count))
    stratum_here = stratum[0]
    masked = token_level * STRATA < (stratum_here + 1) * LEVELS
    loss_weight = jnp.where(
        masked, STRATA / (stratum_here + 1).astype(jnp.float32), jnp.float32(0.0)
    )
    upstream = (cotangent.astype(jnp.float32) * loss_weight[:, None]).astype(jnp.bfloat16)
    chosen = experts.reshape(-1)
    pair_count = chosen.shape[0]
    onehot = (chosen[:, None] == jnp.arange(device_count, dtype=jnp.int32)[None, :]).astype(
        jnp.int32
    )
    ranking = jnp.sum((jnp.cumsum(onehot, axis=0) - 1) * onehot, axis=1)
    placed = chosen * capacity + ranking
    owner_table = jnp.full((device_count * capacity,), pair_count, jnp.int32)
    owner_table = owner_table.at[placed].set(jnp.arange(pair_count, dtype=jnp.int32))
    token_index = (owner_table // chosen_count).reshape(device_count, capacity)
    padded_tokens = jnp.concatenate([tokens, jnp.zeros((1, width), jnp.bfloat16)], axis=0)
    padded_upstream = jnp.concatenate([upstream, jnp.zeros((1, width), jnp.bfloat16)], axis=0)
    weight_in = w_gate_up[0]
    weight_out = w_down[0]
    sizes = CHUNK_SIZES if sum(CHUNK_SIZES) == capacity else (capacity,)
    starts = [sum(sizes[:c]) for c in range(len(sizes))]
    tiled = all((n * width) % (16 * 128) == 0 for n in sizes)
    rows = 16 if tiled else 1

    def block_of(n):
        return (device_count, rows, n * width // rows)

    def exchange(part):
        return lax.all_to_all(part, axes, 0, 0, tiled=True)

    def send_of(c):
        index = token_index[:, starts[c] : starts[c] + sizes[c]].reshape(-1)
        return jnp.concatenate(
            [
                padded_tokens[index].reshape(block_of(sizes[c])),
                padded_upstream[index].reshape(block_of(sizes[c])),
            ],
            axis=1,
        )

    def compute(c, arrived):
        n = sizes[c]
        row_grads, prob_grad = expert_grads(
            arrived[:, :rows].reshape(device_count * n, width),
            arrived[:, rows:].reshape(device_count * n, width),
            weight_in,
            weight_out,
        )
        return row_grads.reshape(block_of(n)), prob_grad.reshape(device_count, n)

    def combine(c, home):
        n = sizes[c]
        local = ranking - starts[c]
        inside = (local >= 0) & (local < n)
        slot = jnp.where(inside, chosen * n + local, -1).reshape(token_rows, chosen_count)
        weight = jnp.where(inside.reshape(token_rows, chosen_count), gate_probs, 0.0)
        table = jnp.sum(
            jnp.where(
                slot[:, :, None] == jnp.arange(device_count * n, dtype=jnp.int32)[None, None, :],
                weight[:, :, None],
                0.0,
            ),
            axis=1,
        )
        high = table.astype(jnp.bfloat16)
        low = (table - high.astype(jnp.float32)).astype(jnp.bfloat16)
        home = home.reshape(device_count * n, width)
        return jnp.dot(high, home, preferred_element_type=jnp.float32) + jnp.dot(
            low, home, preferred_element_type=jnp.float32
        )

    last = len(sizes) - 1
    extra = rows * 128 if rows * 128 >= capacity else capacity
    extra_cols = extra // rows

    arrived = exchange(send_of(0))
    grad_tokens = None
    prob_parts = []
    pending = None
    for c in range(len(sizes)):
        row_grads, prob_grad = compute(c, arrived)
        prob_parts.append(prob_grad)
        if c < last:
            arrived = exchange(send_of(c + 1))
            arrived, row_grads, prob_parts = lax.optimization_barrier(
                (arrived, row_grads, prob_parts)
            )
        if pending is not None:
            pending, row_grads, prob_parts = lax.optimization_barrier(
                (pending, row_grads, prob_parts)
            )
            part = combine(c - 1, pending)
            grad_tokens = part if grad_tokens is None else grad_tokens + part
        if c < last:
            pending = exchange(row_grads)
        else:
            probs = jnp.concatenate(prob_parts, axis=1)
            probs = jnp.pad(probs, ((0, 0), (0, extra - capacity))).reshape(
                device_count, rows, extra_cols
            )
            pending = exchange(jnp.concatenate([row_grads, probs], axis=2))
    row_cols = sizes[last] * width // rows
    part = combine(last, pending[:, :, :row_cols])
    grad_tokens = part if grad_tokens is None else grad_tokens + part
    home_probs = pending[:, :, row_cols:].reshape(device_count, extra)[:, :capacity].reshape(-1)
    grad_probs = home_probs[placed].reshape(token_rows, chosen_count)
    return (grad_tokens.astype(jnp.bfloat16), grad_probs)


def solution(mesh):
    placed = (
        P(("node", "local"), None),
        P(("node", "local"), None),
        P(("node", "local"), None),
        P(("node", "local"), None),
        P(("node", "local")),
        P(("node", "local")),
        P(("node", "local"), None, None),
        P(("node", "local"), None, None),
    )
    return jax.shard_map(
        body,
        mesh=mesh,
        in_specs=placed,
        out_specs=(P(("node", "local"), None), P(("node", "local"), None)),
        check_vma=False,
    )
```

```python
import jax
import jax.numpy as jnp
from jax import lax
from jax.sharding import PartitionSpec as P

STRATA = 8
LEVELS = 64
CHUNK_SIZES = (3, 4, 3)


def expert_grads(inputs, upstream, weight_in, weight_out):
    hidden_units = weight_out.shape[0]
    projected = jnp.dot(inputs, weight_in, preferred_element_type=jnp.float32)
    gate_part = projected[:, :hidden_units]
    up_part = projected[:, hidden_units:]
    sigmoid_gate = jax.nn.sigmoid(gate_part)
    activated = gate_part * sigmoid_gate
    hidden = (activated * up_part).astype(jnp.bfloat16)
    backward = jnp.dot(upstream, weight_out.T, preferred_element_type=jnp.float32)
    prob_grad = jnp.sum(hidden.astype(jnp.float32) * backward, axis=1).astype(jnp.bfloat16)
    grad_gate = backward * up_part * sigmoid_gate * (1.0 + gate_part * (1.0 - sigmoid_gate))
    grad_up = backward * activated
    stacked = jnp.concatenate([grad_gate, grad_up], axis=1).astype(jnp.bfloat16)
    row_grads = jnp.dot(stacked, weight_in.T, preferred_element_type=jnp.float32).astype(
        jnp.bfloat16
    )
    return (row_grads, prob_grad)


def body(tokens, cotangent, gate_probs, experts, stratum, token_level, w_gate_up, w_down):
    axes = ("node", "local")
    device_count = lax.axis_size(axes)
    token_rows, chosen_count = experts.shape
    width = tokens.shape[1]
    capacity = max(2, token_rows * chosen_count * 5 // (4 * device_count))
    stratum_here = stratum[0]
    masked = token_level * STRATA < (stratum_here + 1) * LEVELS
    loss_weight = jnp.where(
        masked, STRATA / (stratum_here + 1).astype(jnp.float32), jnp.float32(0.0)
    )
    upstream = (cotangent.astype(jnp.float32) * loss_weight[:, None]).astype(jnp.bfloat16)
    chosen = experts.reshape(-1)
    pair_count = chosen.shape[0]
    onehot = (chosen[:, None] == jnp.arange(device_count, dtype=jnp.int32)[None, :]).astype(
        jnp.int32
    )
    ranking = jnp.sum((jnp.cumsum(onehot, axis=0) - 1) * onehot, axis=1)
    placed = chosen * capacity + ranking
    owner_table = jnp.full((device_count * capacity,), pair_count, jnp.int32)
    owner_table = owner_table.at[placed].set(jnp.arange(pair_count, dtype=jnp.int32))
    token_index = (owner_table // chosen_count).reshape(device_count, capacity)
    padded_tokens = jnp.concatenate([tokens, jnp.zeros((1, width), jnp.bfloat16)], axis=0)
    padded_upstream = jnp.concatenate([upstream, jnp.zeros((1, width), jnp.bfloat16)], axis=0)
    weight_in = w_gate_up[0]
    weight_out = w_down[0]
    sizes = CHUNK_SIZES if sum(CHUNK_SIZES) == capacity else (capacity,)
    starts = [sum(sizes[:c]) for c in range(len(sizes))]
    tiled = all((n * width) % (16 * 128) == 0 for n in sizes)
    rows = 16 if tiled else 1

    def block_of(n):
        return (device_count, rows, n * width // rows)

    def exchange(part):
        return lax.all_to_all(part, axes, 0, 0, tiled=True)

    sources = jnp.concatenate([padded_tokens, padded_upstream], axis=0)

    def send_of(c):
        index = token_index[:, starts[c] : starts[c] + sizes[c]]
        index = jnp.stack([index, index + (token_rows + 1)], axis=1).reshape(-1)
        return sources[index].reshape(device_count, 2 * rows, sizes[c] * width // rows)

    def compute(c, arrived):
        n = sizes[c]
        row_grads, prob_grad = expert_grads(
            arrived[:, :rows].reshape(device_count * n, width),
            arrived[:, rows:].reshape(device_count * n, width),
            weight_in,
            weight_out,
        )
        return row_grads.reshape(block_of(n)), prob_grad.reshape(device_count, n)

    def combine(c, home):
        n = sizes[c]
        local = ranking - starts[c]
        inside = (local >= 0) & (local < n)
        slot = jnp.where(inside, chosen * n + local, -1).reshape(token_rows, chosen_count)
        weight = jnp.where(inside.reshape(token_rows, chosen_count), gate_probs, 0.0)
        table = jnp.sum(
            jnp.where(
                slot[:, :, None] == jnp.arange(device_count * n, dtype=jnp.int32)[None, None, :],
                weight[:, :, None],
                0.0,
            ),
            axis=1,
        )
        high = table.astype(jnp.bfloat16)
        low = (table - high.astype(jnp.float32)).astype(jnp.bfloat16)
        home = home.reshape(device_count * n, width)
        return jnp.dot(high, home, preferred_element_type=jnp.float32) + jnp.dot(
            low, home, preferred_element_type=jnp.float32
        )

    last = len(sizes) - 1
    extra = rows * 128 if rows * 128 >= capacity else capacity
    extra_cols = extra // rows

    arrived = exchange(send_of(0))
    grad_tokens = None
    prob_parts = []
    pending = None
    for c in range(len(sizes)):
        row_grads, prob_grad = compute(c, arrived)
        prob_parts.append(prob_grad)
        if c < last:
            arrived = exchange(send_of(c + 1))
            arrived, row_grads, prob_parts = lax.optimization_barrier(
                (arrived, row_grads, prob_parts)
            )
        if pending is not None:
            pending, row_grads, prob_parts = lax.optimization_barrier(
                (pending, row_grads, prob_parts)
            )
            part = combine(c - 1, pending)
            grad_tokens = part if grad_tokens is None else grad_tokens + part
        if c < last:
            pending = exchange(row_grads)
        else:
            probs = jnp.concatenate(prob_parts, axis=1)
            probs = jnp.pad(probs, ((0, 0), (0, extra - capacity))).reshape(
                device_count, rows, extra_cols
            )
            pending = exchange(jnp.concatenate([row_grads, probs], axis=2))
    row_cols = sizes[last] * width // rows
    part = combine(last, pending[:, :, :row_cols])
    grad_tokens = part if grad_tokens is None else grad_tokens + part
    home_probs = pending[:, :, row_cols:].reshape(device_count, extra)[:, :capacity].reshape(-1)
    pick = placed[:, None] == jnp.arange(device_count * capacity, dtype=jnp.int32)[None, :]
    grad_probs = jnp.sum(
        jnp.where(pick, home_probs.astype(jnp.float32)[None, :], 0.0), axis=1
    ).astype(jnp.bfloat16)
    grad_probs = grad_probs.reshape(token_rows, chosen_count)
    return (grad_tokens.astype(jnp.bfloat16), grad_probs)


def solution(mesh):
    placed = (
        P(("node", "local"), None),
        P(("node", "local"), None),
        P(("node", "local"), None),
        P(("node", "local"), None),
        P(("node", "local")),
        P(("node", "local")),
        P(("node", "local"), None, None),
        P(("node", "local"), None, None),
    )
    return jax.shard_map(
        body,
        mesh=mesh,
        in_specs=placed,
        out_specs=(P(("node", "local"), None), P(("node", "local"), None)),
        check_vma=False,
    )
```

```python
import jax
import jax.numpy as jnp
from jax import lax
from jax.sharding import PartitionSpec as P

STRATA = 8
LEVELS = 64
CHUNK_SIZES = (3, 4, 3)


def expert_grads(inputs, upstream, weight_in, weight_out):
    hidden_units = weight_out.shape[0]
    projected = jnp.dot(inputs, weight_in, preferred_element_type=jnp.float32)
    gate_part = projected[:, :hidden_units]
    up_part = projected[:, hidden_units:]
    sigmoid_gate = jax.nn.sigmoid(gate_part)
    activated = gate_part * sigmoid_gate
    hidden = (activated * up_part).astype(jnp.bfloat16)
    backward = jnp.dot(upstream, weight_out.T, preferred_element_type=jnp.float32)
    prob_grad = jnp.sum(hidden.astype(jnp.float32) * backward, axis=1).astype(jnp.bfloat16)
    grad_gate = backward * up_part * sigmoid_gate * (1.0 + gate_part * (1.0 - sigmoid_gate))
    grad_up = backward * activated
    stacked = jnp.concatenate([grad_gate, grad_up], axis=1).astype(jnp.bfloat16)
    row_grads = jnp.dot(stacked, weight_in.T, preferred_element_type=jnp.float32).astype(
        jnp.bfloat16
    )
    return (row_grads, prob_grad)


def body(tokens, cotangent, gate_probs, experts, stratum, token_level, w_gate_up, w_down):
    axes = ("node", "local")
    device_count = lax.axis_size(axes)
    token_rows, chosen_count = experts.shape
    width = tokens.shape[1]
    capacity = max(2, token_rows * chosen_count * 5 // (4 * device_count))
    stratum_here = stratum[0]
    masked = token_level * STRATA < (stratum_here + 1) * LEVELS
    loss_weight = jnp.where(
        masked, STRATA / (stratum_here + 1).astype(jnp.float32), jnp.float32(0.0)
    )
    upstream = (cotangent.astype(jnp.float32) * loss_weight[:, None]).astype(jnp.bfloat16)
    chosen = experts.reshape(-1)
    pair_count = chosen.shape[0]
    onehot = (chosen[:, None] == jnp.arange(device_count, dtype=jnp.int32)[None, :]).astype(
        jnp.int32
    )
    ranking = jnp.sum((jnp.cumsum(onehot, axis=0) - 1) * onehot, axis=1)
    placed = chosen * capacity + ranking
    owner_table = jnp.full((device_count * capacity,), pair_count, jnp.int32)
    owner_table = owner_table.at[placed].set(jnp.arange(pair_count, dtype=jnp.int32))
    token_index = (owner_table // chosen_count).reshape(device_count, capacity)
    padded_tokens = jnp.concatenate([tokens, jnp.zeros((1, width), jnp.bfloat16)], axis=0)
    padded_upstream = jnp.concatenate([upstream, jnp.zeros((1, width), jnp.bfloat16)], axis=0)
    weight_in = w_gate_up[0]
    weight_out = w_down[0]
    sizes = CHUNK_SIZES if sum(CHUNK_SIZES) == capacity else (capacity,)
    starts = [sum(sizes[:c]) for c in range(len(sizes))]
    tiled = all((n * width) % (16 * 128) == 0 for n in sizes)
    rows = 16 if tiled else 1

    def block_of(n):
        return (device_count, rows, n * width // rows)

    def exchange(part):
        return lax.all_to_all(part, axes, 0, 0, tiled=True)

    sources = jnp.concatenate([padded_tokens, padded_upstream], axis=0)

    def send_of(c):
        index = token_index[:, starts[c] : starts[c] + sizes[c]]
        index = jnp.stack([index, index + (token_rows + 1)], axis=1).reshape(-1)
        return sources[index].reshape(device_count, 2 * rows, sizes[c] * width // rows)

    def compute(c, arrived):
        n = sizes[c]
        row_grads, prob_grad = expert_grads(
            arrived[:, :rows].reshape(device_count * n, width),
            arrived[:, rows:].reshape(device_count * n, width),
            weight_in,
            weight_out,
        )
        return row_grads.reshape(block_of(n)), prob_grad.reshape(device_count, n)

    def combine(c, home):
        n = sizes[c]
        local = ranking - starts[c]
        inside = (local >= 0) & (local < n)
        slot = jnp.where(inside, chosen * n + local, -1).reshape(token_rows, chosen_count)
        weight = jnp.where(inside.reshape(token_rows, chosen_count), gate_probs, 0.0)
        table = jnp.sum(
            jnp.where(
                slot[:, :, None] == jnp.arange(device_count * n, dtype=jnp.int32)[None, None, :],
                weight[:, :, None],
                0.0,
            ),
            axis=1,
        )
        high = table.astype(jnp.bfloat16)
        low = (table - high.astype(jnp.float32)).astype(jnp.bfloat16)
        home = home.reshape(device_count * n, width)
        return jnp.dot(high, home, preferred_element_type=jnp.float32) + jnp.dot(
            low, home, preferred_element_type=jnp.float32
        )

    last = len(sizes) - 1
    extra = rows * 128 if rows * 128 >= capacity else capacity
    extra_cols = extra // rows

    order = [("S", 0)]
    for c in range(1, len(sizes)):
        order += [("S", c), ("R", c - 1)]
    order.append(("R", last))
    arrived = {}
    returned = {}
    row_grads = {}
    prob_parts = {}
    grad_tokens = None
    previous = None
    for k, (kind, c) in enumerate(order):
        if kind == "S":
            buffer = send_of(c)
        elif c < last:
            buffer = row_grads[c]
        else:
            probs = jnp.concatenate([prob_parts[i] for i in range(len(sizes))], axis=1)
            probs = jnp.pad(probs, ((0, 0), (0, extra - capacity))).reshape(
                device_count, rows, extra_cols
            )
            buffer = jnp.concatenate([row_grads[c], probs], axis=2)
        if previous is not None:
            buffer, previous = lax.optimization_barrier((buffer, previous))
        done = exchange(buffer)
        covered = []
        if k + 1 < len(order) and order[k + 1][0] == "R":
            n = order[k + 1][1]
            row_grads[n], prob_parts[n] = compute(n, arrived[n])
            covered += [row_grads[n], prob_parts[n]]
        if k >= 1 and order[k - 1][0] == "R" and order[k - 1][1] < last:
            n = order[k - 1][1]
            part = combine(n, returned[n])
            grad_tokens = part if grad_tokens is None else grad_tokens + part
            covered.append(grad_tokens)
        if covered:
            done, covered = lax.optimization_barrier((done, covered))
            i = 0
            if k + 1 < len(order) and order[k + 1][0] == "R":
                n = order[k + 1][1]
                row_grads[n], prob_parts[n] = covered[0], covered[1]
                i = 2
            if k >= 1 and order[k - 1][0] == "R" and order[k - 1][1] < last:
                grad_tokens = covered[i]
        if kind == "S":
            arrived[c] = done
        else:
            returned[c] = done
        previous = done
    pending = returned[last]
    row_cols = sizes[last] * width // rows
    part = combine(last, pending[:, :, :row_cols])
    grad_tokens = part if grad_tokens is None else grad_tokens + part
    home_probs = pending[:, :, row_cols:].reshape(device_count, extra)[:, :capacity].reshape(-1)
    pick = placed[:, None] == jnp.arange(device_count * capacity, dtype=jnp.int32)[None, :]
    grad_probs = jnp.sum(
        jnp.where(pick, home_probs.astype(jnp.float32)[None, :], 0.0), axis=1
    ).astype(jnp.bfloat16)
    grad_probs = grad_probs.reshape(token_rows, chosen_count)
    return (grad_tokens.astype(jnp.bfloat16), grad_probs)


def solution(mesh):
    placed = (
        P(("node", "local"), None),
        P(("node", "local"), None),
        P(("node", "local"), None),
        P(("node", "local"), None),
        P(("node", "local")),
        P(("node", "local")),
        P(("node", "local"), None, None),
        P(("node", "local"), None, None),
    )
    return jax.shard_map(
        body,
        mesh=mesh,
        in_specs=placed,
        out_specs=(P(("node", "local"), None), P(("node", "local"), None)),
        check_vma=False,
    )
```

```python
import jax
import jax.numpy as jnp
from jax import lax
from jax.sharding import PartitionSpec as P

STRATA = 8
LEVELS = 64
CHUNK_SIZES = (3, 4, 3)


def expert_grads(inputs, upstream, weight_in, weight_out):
    hidden_units = weight_out.shape[0]
    projected = jnp.dot(inputs, weight_in, preferred_element_type=jnp.float32)
    gate_part = projected[:, :hidden_units]
    up_part = projected[:, hidden_units:]
    sigmoid_gate = jax.nn.sigmoid(gate_part)
    activated = gate_part * sigmoid_gate
    hidden = (activated * up_part).astype(jnp.bfloat16)
    backward = jnp.dot(upstream, weight_out.T, preferred_element_type=jnp.float32)
    prob_grad = jnp.sum(hidden.astype(jnp.float32) * backward, axis=1).astype(jnp.bfloat16)
    grad_gate = backward * up_part * sigmoid_gate * (1.0 + gate_part * (1.0 - sigmoid_gate))
    grad_up = backward * activated
    stacked = jnp.concatenate([grad_gate, grad_up], axis=1).astype(jnp.bfloat16)
    row_grads = jnp.dot(stacked, weight_in.T, preferred_element_type=jnp.float32).astype(
        jnp.bfloat16
    )
    return (row_grads, prob_grad)


def body(tokens, cotangent, gate_probs, experts, stratum, token_level, w_gate_up, w_down):
    axes = ("node", "local")
    device_count = lax.axis_size(axes)
    token_rows, chosen_count = experts.shape
    width = tokens.shape[1]
    capacity = max(2, token_rows * chosen_count * 5 // (4 * device_count))
    stratum_here = stratum[0]
    masked = token_level * STRATA < (stratum_here + 1) * LEVELS
    loss_weight = jnp.where(
        masked, STRATA / (stratum_here + 1).astype(jnp.float32), jnp.float32(0.0)
    )
    upstream = (cotangent.astype(jnp.float32) * loss_weight[:, None]).astype(jnp.bfloat16)
    chosen = experts.reshape(-1)
    pair_count = chosen.shape[0]
    onehot = (chosen[:, None] == jnp.arange(device_count, dtype=jnp.int32)[None, :]).astype(
        jnp.int32
    )
    ranking = jnp.sum((jnp.cumsum(onehot, axis=0) - 1) * onehot, axis=1)
    placed = chosen * capacity + ranking
    owner_table = jnp.full((device_count * capacity,), pair_count, jnp.int32)
    owner_table = owner_table.at[placed].set(jnp.arange(pair_count, dtype=jnp.int32))
    token_index = (owner_table // chosen_count).reshape(device_count, capacity)
    padded_tokens = jnp.concatenate([tokens, jnp.zeros((1, width), jnp.bfloat16)], axis=0)
    padded_upstream = jnp.concatenate([upstream, jnp.zeros((1, width), jnp.bfloat16)], axis=0)
    weight_in = w_gate_up[0]
    weight_out = w_down[0]
    sizes = CHUNK_SIZES if sum(CHUNK_SIZES) == capacity else (capacity,)
    starts = [sum(sizes[:c]) for c in range(len(sizes))]
    tiled = all((n * width) % (16 * 128) == 0 for n in sizes)
    rows = 16 if tiled else 1

    def block_of(n):
        return (device_count, rows, n * width // rows)

    def exchange(part):
        return lax.all_to_all(part, axes, 0, 0, tiled=True)

    sources = jnp.concatenate([padded_tokens, padded_upstream], axis=0)

    def send_of(c):
        index = token_index[:, starts[c] : starts[c] + sizes[c]]
        index = jnp.stack([index, index + (token_rows + 1)], axis=1).reshape(-1)
        return sources[index].reshape(device_count, 2 * rows, sizes[c] * width // rows)

    def compute(c, arrived):
        n = sizes[c]
        row_grads, prob_grad = expert_grads(
            arrived[:, :rows].reshape(device_count * n, width),
            arrived[:, rows:].reshape(device_count * n, width),
            weight_in,
            weight_out,
        )
        return row_grads.reshape(block_of(n)), prob_grad.reshape(device_count, n)

    def combine(c, home):
        n = sizes[c]
        local = ranking - starts[c]
        inside = (local >= 0) & (local < n)
        slot = jnp.where(inside, chosen * n + local, -1).reshape(token_rows, chosen_count)
        weight = jnp.where(inside.reshape(token_rows, chosen_count), gate_probs, 0.0)
        table = jnp.sum(
            jnp.where(
                slot[:, :, None] == jnp.arange(device_count * n, dtype=jnp.int32)[None, None, :],
                weight[:, :, None],
                0.0,
            ),
            axis=1,
        )
        high = table.astype(jnp.bfloat16)
        low = (table - high.astype(jnp.float32)).astype(jnp.bfloat16)
        home = home.reshape(device_count * n, width)
        return jnp.dot(high, home, preferred_element_type=jnp.float32) + jnp.dot(
            low, home, preferred_element_type=jnp.float32
        )

    last = len(sizes) - 1
    extra = rows * 128 if rows * 128 >= capacity else capacity
    extra_cols = extra // rows

    order = [((), (0,))]
    if last >= 1:
        order.append(((), (1,)))
    for c in range(2, len(sizes)):
        if sizes[c - 2] == sizes[c]:
            order.append(((c - 2,), (c,)))
        else:
            order += [((c - 2,), ()), ((), (c,))]
    for c in range(max(0, len(sizes) - 2), len(sizes)):
        order.append(((c,), ()))

    def final_block():
        probs = jnp.concatenate([prob_parts[i] for i in range(len(sizes))], axis=1)
        probs = jnp.pad(probs, ((0, 0), (0, extra - capacity))).reshape(
            device_count, rows, extra_cols
        )
        return jnp.concatenate([row_grads[last], probs], axis=2)

    arrived = {}
    returned = {}
    row_grads = {}
    prob_parts = {}

    def buffer_of(k):
        backs, sends = order[k]
        parts = [final_block() if n == last else row_grads[n] for n in backs]
        parts += [send_of(n) for n in sends]
        return parts[0] if len(parts) == 1 else jnp.concatenate(parts, axis=1)

    grad_tokens = None
    buffer = buffer_of(0)
    for k, (backs, sends) in enumerate(order):
        done = exchange(buffer)
        computed = [n for n in (order[k + 1][0] if k + 1 < len(order) else ())]
        combined = [n for n in (order[k - 1][0] if k >= 1 else ()) if n < last]
        for n in computed:
            row_grads[n], prob_parts[n] = compute(n, arrived[n])
        for n in combined:
            part = combine(n, returned[n])
            grad_tokens = part if grad_tokens is None else grad_tokens + part
        buffer = buffer_of(k + 1) if k + 1 < len(order) else None
        covered = (buffer, grad_tokens if combined else None)
        done, covered = lax.optimization_barrier((done, covered))
        buffer = covered[0]
        if combined:
            grad_tokens = covered[1]
        offset = 0
        for n in backs:
            returned[n] = done[:, offset : offset + rows] if len(backs) + len(sends) > 1 else done
            offset += rows
        for n in sends:
            arrived[n] = done[:, offset : offset + 2 * rows] if len(backs) + len(sends) > 1 else done
            offset += 2 * rows
    pending = returned[last]
    row_cols = sizes[last] * width // rows
    part = combine(last, pending[:, :, :row_cols])
    grad_tokens = part if grad_tokens is None else grad_tokens + part
    home_probs = pending[:, :, row_cols:].reshape(device_count, extra)[:, :capacity].reshape(-1)
    pick = placed[:, None] == jnp.arange(device_count * capacity, dtype=jnp.int32)[None, :]
    grad_probs = jnp.sum(
        jnp.where(pick, home_probs.astype(jnp.float32)[None, :], 0.0), axis=1
    ).astype(jnp.bfloat16)
    grad_probs = grad_probs.reshape(token_rows, chosen_count)
    return (grad_tokens.astype(jnp.bfloat16), grad_probs)


def solution(mesh):
    placed = (
        P(("node", "local"), None),
        P(("node", "local"), None),
        P(("node", "local"), None),
        P(("node", "local"), None),
        P(("node", "local")),
        P(("node", "local")),
        P(("node", "local"), None, None),
        P(("node", "local"), None, None),
    )
    return jax.shard_map(
        body,
        mesh=mesh,
        in_specs=placed,
        out_specs=(P(("node", "local"), None), P(("node", "local"), None)),
        check_vma=False,
    )
```

```python
import jax
import jax.numpy as jnp
from jax import lax
from jax.sharding import PartitionSpec as P

STRATA = 8
LEVELS = 64
CHUNK_SIZES = (3, 4, 3)


def expert_grads(inputs, upstream, weight_in, weight_out):
    hidden_units = weight_out.shape[0]
    projected = jnp.dot(inputs, weight_in, preferred_element_type=jnp.float32)
    gate_part = projected[:, :hidden_units]
    up_part = projected[:, hidden_units:]
    sigmoid_gate = jax.nn.sigmoid(gate_part)
    activated = gate_part * sigmoid_gate
    hidden = (activated * up_part).astype(jnp.bfloat16)
    backward = jnp.dot(upstream, weight_out.T, preferred_element_type=jnp.float32)
    prob_grad = jnp.sum(hidden.astype(jnp.float32) * backward, axis=1).astype(jnp.bfloat16)
    grad_gate = backward * up_part * sigmoid_gate * (1.0 + gate_part * (1.0 - sigmoid_gate))
    grad_up = backward * activated
    stacked = jnp.concatenate([grad_gate, grad_up], axis=1).astype(jnp.bfloat16)
    row_grads = jnp.dot(stacked, weight_in.T, preferred_element_type=jnp.float32).astype(
        jnp.bfloat16
    )
    return (row_grads, prob_grad)


def body(tokens, cotangent, gate_probs, experts, stratum, token_level, w_gate_up, w_down):
    axes = ("node", "local")
    device_count = lax.axis_size(axes)
    token_rows, chosen_count = experts.shape
    width = tokens.shape[1]
    capacity = max(2, token_rows * chosen_count * 5 // (4 * device_count))
    stratum_here = stratum[0]
    masked = token_level * STRATA < (stratum_here + 1) * LEVELS
    loss_weight = jnp.where(
        masked, STRATA / (stratum_here + 1).astype(jnp.float32), jnp.float32(0.0)
    )
    upstream = (cotangent.astype(jnp.float32) * loss_weight[:, None]).astype(jnp.bfloat16)
    chosen = experts.reshape(-1)
    pair_count = chosen.shape[0]
    onehot = (chosen[:, None] == jnp.arange(device_count, dtype=jnp.int32)[None, :]).astype(
        jnp.int32
    )
    ranking = jnp.sum((jnp.cumsum(onehot, axis=0) - 1) * onehot, axis=1)
    placed = chosen * capacity + ranking
    owner_table = jnp.full((device_count * capacity,), pair_count, jnp.int32)
    owner_table = owner_table.at[placed].set(jnp.arange(pair_count, dtype=jnp.int32))
    token_index = (owner_table // chosen_count).reshape(device_count, capacity)
    padded_tokens = jnp.concatenate([tokens, jnp.zeros((1, width), jnp.bfloat16)], axis=0)
    padded_upstream = jnp.concatenate([upstream, jnp.zeros((1, width), jnp.bfloat16)], axis=0)
    weight_in = w_gate_up[0]
    weight_out = w_down[0]
    sizes = CHUNK_SIZES if sum(CHUNK_SIZES) == capacity else (capacity,)
    starts = [sum(sizes[:c]) for c in range(len(sizes))]
    tiled = all((n * width) % (16 * 128) == 0 for n in sizes)
    rows = 16 if tiled else 1

    def block_of(n):
        return (device_count, rows, n * width // rows)

    def exchange(part):
        return lax.all_to_all(part, axes, 0, 0, tiled=True)

    sources = jnp.concatenate([padded_tokens, padded_upstream], axis=0)

    def send_of(c):
        index = token_index[:, starts[c] : starts[c] + sizes[c]]
        index = jnp.stack([index, index + (token_rows + 1)], axis=1).reshape(-1)
        return sources[index].reshape(device_count, 2 * rows, sizes[c] * width // rows)

    def compute(c, arrived):
        n = sizes[c]
        row_grads, prob_grad = expert_grads(
            arrived[:, :rows].reshape(device_count * n, width),
            arrived[:, rows:].reshape(device_count * n, width),
            weight_in,
            weight_out,
        )
        return row_grads.reshape(block_of(n)), prob_grad.reshape(device_count, n)

    def combine(c, home):
        n = sizes[c]
        local = ranking - starts[c]
        inside = (local >= 0) & (local < n)
        slot = jnp.where(inside, chosen * n + local, -1).reshape(token_rows, chosen_count)
        weight = jnp.where(inside.reshape(token_rows, chosen_count), gate_probs, 0.0)
        table = jnp.sum(
            jnp.where(
                slot[:, :, None] == jnp.arange(device_count * n, dtype=jnp.int32)[None, None, :],
                weight[:, :, None],
                0.0,
            ),
            axis=1,
        )
        high = table.astype(jnp.bfloat16)
        low = (table - high.astype(jnp.float32)).astype(jnp.bfloat16)
        home = home.reshape(device_count * n, width)
        return jnp.dot(high, home, preferred_element_type=jnp.float32) + jnp.dot(
            low, home, preferred_element_type=jnp.float32
        )

    last = len(sizes) - 1
    extra = rows * 128 if rows * 128 >= capacity else capacity
    extra_cols = extra // rows

    order = [((), (0,))]
    if last >= 1:
        order.append(((), (1,)))
    for c in range(2, len(sizes)):
        if sizes[c - 2] == sizes[c]:
            order.append(((c - 2,), (c,)))
        else:
            order += [((c - 2,), ()), ((), (c,))]
    for c in range(max(0, len(sizes) - 2), len(sizes)):
        order.append(((c,), ()))

    def final_block():
        probs = jnp.concatenate([prob_parts[i] for i in range(len(sizes))], axis=1)
        probs = jnp.pad(probs, ((0, 0), (0, extra - capacity))).reshape(
            device_count, rows, extra_cols
        )
        return jnp.concatenate([row_grads[last], probs], axis=2)

    arrived = {}
    returned = {}
    row_grads = {}
    prob_parts = {}

    def buffer_of(k):
        backs, sends = order[k]
        parts = [final_block() if n == last else row_grads[n] for n in backs]
        parts += [send_of(n) for n in sends]
        return parts[0] if len(parts) == 1 else jnp.concatenate(parts, axis=1)

    grad_tokens = None
    summed = set()
    buffer = buffer_of(0)
    for k, (backs, sends) in enumerate(order):
        done = exchange(buffer)
        computed = [n for n in (order[k + 1][0] if k + 1 < len(order) else ())]
        combined = []
        if not computed:
            combined = [n for n in sorted(returned) if n < last and n not in summed]
            summed.update(combined)
        for n in computed:
            row_grads[n], prob_parts[n] = compute(n, arrived[n])
        for n in combined:
            part = combine(n, returned[n])
            grad_tokens = part if grad_tokens is None else grad_tokens + part
        buffer = buffer_of(k + 1) if k + 1 < len(order) else None
        covered = (buffer, grad_tokens if combined else None)
        done, covered = lax.optimization_barrier((done, covered))
        buffer = covered[0]
        if combined:
            grad_tokens = covered[1]
        offset = 0
        for n in backs:
            returned[n] = done[:, offset : offset + rows] if len(backs) + len(sends) > 1 else done
            offset += rows
        for n in sends:
            arrived[n] = done[:, offset : offset + 2 * rows] if len(backs) + len(sends) > 1 else done
            offset += 2 * rows
    pending = returned[last]
    row_cols = sizes[last] * width // rows
    part = combine(last, pending[:, :, :row_cols])
    grad_tokens = part if grad_tokens is None else grad_tokens + part
    home_probs = pending[:, :, row_cols:].reshape(device_count, extra)[:, :capacity].reshape(-1)
    pick = placed[:, None] == jnp.arange(device_count * capacity, dtype=jnp.int32)[None, :]
    grad_probs = jnp.sum(
        jnp.where(pick, home_probs.astype(jnp.float32)[None, :], 0.0), axis=1
    ).astype(jnp.bfloat16)
    grad_probs = grad_probs.reshape(token_rows, chosen_count)
    return (grad_tokens.astype(jnp.bfloat16), grad_probs)


def solution(mesh):
    placed = (
        P(("node", "local"), None),
        P(("node", "local"), None),
        P(("node", "local"), None),
        P(("node", "local"), None),
        P(("node", "local")),
        P(("node", "local")),
        P(("node", "local"), None, None),
        P(("node", "local"), None, None),
    )
    return jax.shard_map(
        body,
        mesh=mesh,
        in_specs=placed,
        out_specs=(P(("node", "local"), None), P(("node", "local"), None)),
        check_vma=False,
    )
```

```python
import jax
import jax.numpy as jnp
from jax import lax
from jax.sharding import PartitionSpec as P

STRATA = 8
LEVELS = 64
CHUNK_SIZES = (3, 4, 3)


def expert_grads(inputs, upstream, weight_in, weight_out):
    hidden_units = weight_out.shape[0]
    projected = jnp.dot(inputs, weight_in, preferred_element_type=jnp.float32)
    gate_part = projected[:, :hidden_units]
    up_part = projected[:, hidden_units:]
    sigmoid_gate = jax.nn.sigmoid(gate_part)
    activated = gate_part * sigmoid_gate
    hidden = (activated * up_part).astype(jnp.bfloat16)
    backward = jnp.dot(upstream, weight_out.T, preferred_element_type=jnp.float32)
    prob_grad = jnp.sum(hidden.astype(jnp.float32) * backward, axis=1).astype(jnp.bfloat16)
    grad_gate = backward * up_part * sigmoid_gate * (1.0 + gate_part * (1.0 - sigmoid_gate))
    grad_up = backward * activated
    stacked = jnp.concatenate([grad_gate, grad_up], axis=1).astype(jnp.bfloat16)
    row_grads = jnp.dot(stacked, weight_in.T, preferred_element_type=jnp.float32).astype(
        jnp.bfloat16
    )
    return (row_grads, prob_grad)


def body(tokens, cotangent, gate_probs, experts, stratum, token_level, w_gate_up, w_down):
    axes = ("node", "local")
    device_count = lax.axis_size(axes)
    token_rows, chosen_count = experts.shape
    width = tokens.shape[1]
    capacity = max(2, token_rows * chosen_count * 5 // (4 * device_count))
    stratum_here = stratum[0]
    masked = token_level * STRATA < (stratum_here + 1) * LEVELS
    loss_weight = jnp.where(
        masked, STRATA / (stratum_here + 1).astype(jnp.float32), jnp.float32(0.0)
    )
    upstream = (cotangent.astype(jnp.float32) * loss_weight[:, None]).astype(jnp.bfloat16)
    chosen = experts.reshape(-1)
    pair_count = chosen.shape[0]
    onehot = (chosen[:, None] == jnp.arange(device_count, dtype=jnp.int32)[None, :]).astype(
        jnp.int32
    )
    ranking = jnp.sum((jnp.cumsum(onehot, axis=0) - 1) * onehot, axis=1)
    placed = chosen * capacity + ranking
    holder = placed[None, :] == jnp.arange(device_count * capacity, dtype=jnp.int32)[:, None]
    token_index = jnp.min(
        jnp.where(holder, jnp.arange(pair_count, dtype=jnp.int32)[None, :] // chosen_count, token_rows),
        axis=1,
    ).reshape(device_count, capacity)
    padded_tokens = jnp.concatenate([tokens, jnp.zeros((1, width), jnp.bfloat16)], axis=0)
    padded_upstream = jnp.concatenate([upstream, jnp.zeros((1, width), jnp.bfloat16)], axis=0)
    weight_in = w_gate_up[0]
    weight_out = w_down[0]
    sizes = CHUNK_SIZES if sum(CHUNK_SIZES) == capacity else (capacity,)
    starts = [sum(sizes[:c]) for c in range(len(sizes))]
    tiled = all((n * width) % (16 * 128) == 0 for n in sizes)
    rows = 16 if tiled else 1

    def block_of(n):
        return (device_count, rows, n * width // rows)

    def exchange(part):
        return lax.all_to_all(part, axes, 0, 0, tiled=True)

    sources = jnp.concatenate([padded_tokens, padded_upstream], axis=0)

    def send_of(c):
        index = token_index[:, starts[c] : starts[c] + sizes[c]]
        index = jnp.stack([index, index + (token_rows + 1)], axis=1).reshape(-1)
        return sources[index].reshape(device_count, 2 * rows, sizes[c] * width // rows)

    def compute(c, arrived):
        n = sizes[c]
        row_grads, prob_grad = expert_grads(
            arrived[:, :rows].reshape(device_count * n, width),
            arrived[:, rows:].reshape(device_count * n, width),
            weight_in,
            weight_out,
        )
        return row_grads.reshape(block_of(n)), prob_grad.reshape(device_count, n)

    def combine(c, home):
        n = sizes[c]
        local = ranking - starts[c]
        inside = (local >= 0) & (local < n)
        slot = jnp.where(inside, chosen * n + local, -1).reshape(token_rows, chosen_count)
        weight = jnp.where(inside.reshape(token_rows, chosen_count), gate_probs, 0.0)
        table = jnp.sum(
            jnp.where(
                slot[:, :, None] == jnp.arange(device_count * n, dtype=jnp.int32)[None, None, :],
                weight[:, :, None],
                0.0,
            ),
            axis=1,
        )
        high = table.astype(jnp.bfloat16)
        low = (table - high.astype(jnp.float32)).astype(jnp.bfloat16)
        home = home.reshape(device_count * n, width)
        return jnp.dot(high, home, preferred_element_type=jnp.float32) + jnp.dot(
            low, home, preferred_element_type=jnp.float32
        )

    last = len(sizes) - 1
    extra = rows * 128 if rows * 128 >= capacity else capacity
    extra_cols = extra // rows

    order = [((), (0,))]
    if last >= 1:
        order.append(((), (1,)))
    for c in range(2, len(sizes)):
        if sizes[c - 2] == sizes[c]:
            order.append(((c - 2,), (c,)))
        else:
            order += [((c - 2,), ()), ((), (c,))]
    for c in range(max(0, len(sizes) - 2), len(sizes)):
        order.append(((c,), ()))

    def final_block():
        probs = jnp.concatenate([prob_parts[i] for i in range(len(sizes))], axis=1)
        probs = jnp.pad(probs, ((0, 0), (0, extra - capacity))).reshape(
            device_count, rows, extra_cols
        )
        return jnp.concatenate([row_grads[last], probs], axis=2)

    arrived = {}
    returned = {}
    row_grads = {}
    prob_parts = {}

    def buffer_of(k):
        backs, sends = order[k]
        parts = [final_block() if n == last else row_grads[n] for n in backs]
        parts += [send_of(n) for n in sends]
        return parts[0] if len(parts) == 1 else jnp.concatenate(parts, axis=1)

    grad_tokens = None
    summed = set()
    buffer = buffer_of(0)
    for k, (backs, sends) in enumerate(order):
        done = exchange(buffer)
        computed = [n for n in (order[k + 1][0] if k + 1 < len(order) else ())]
        combined = []
        if not computed:
            combined = [n for n in sorted(returned) if n < last and n not in summed]
            summed.update(combined)
        for n in computed:
            row_grads[n], prob_parts[n] = compute(n, arrived[n])
        for n in combined:
            part = combine(n, returned[n])
            grad_tokens = part if grad_tokens is None else grad_tokens + part
        buffer = buffer_of(k + 1) if k + 1 < len(order) else None
        covered = (buffer, grad_tokens if combined else None)
        done, covered = lax.optimization_barrier((done, covered))
        buffer = covered[0]
        if combined:
            grad_tokens = covered[1]
        offset = 0
        for n in backs:
            returned[n] = done[:, offset : offset + rows] if len(backs) + len(sends) > 1 else done
            offset += rows
        for n in sends:
            arrived[n] = done[:, offset : offset + 2 * rows] if len(backs) + len(sends) > 1 else done
            offset += 2 * rows
    pending = returned[last]
    row_cols = sizes[last] * width // rows
    part = combine(last, pending[:, :, :row_cols])
    grad_tokens = part if grad_tokens is None else grad_tokens + part
    home_probs = pending[:, :, row_cols:].reshape(device_count, extra)[:, :capacity].reshape(-1)
    pick = placed[:, None] == jnp.arange(device_count * capacity, dtype=jnp.int32)[None, :]
    grad_probs = jnp.sum(
        jnp.where(pick, home_probs.astype(jnp.float32)[None, :], 0.0), axis=1
    ).astype(jnp.bfloat16)
    grad_probs = grad_probs.reshape(token_rows, chosen_count)
    return (grad_tokens.astype(jnp.bfloat16), grad_probs)


def solution(mesh):
    placed = (
        P(("node", "local"), None),
        P(("node", "local"), None),
        P(("node", "local"), None),
        P(("node", "local"), None),
        P(("node", "local")),
        P(("node", "local")),
        P(("node", "local"), None, None),
        P(("node", "local"), None, None),
    )
    return jax.shard_map(
        body,
        mesh=mesh,
        in_specs=placed,
        out_specs=(P(("node", "local"), None), P(("node", "local"), None)),
        check_vma=False,
    )
```

```python
import jax
import jax.numpy as jnp
from jax import lax
from jax.sharding import PartitionSpec as P

STRATA = 8
LEVELS = 64
CHUNK_SIZES = (2, 6, 2)


def expert_grads(inputs, upstream, weight_in, weight_out):
    hidden_units = weight_out.shape[0]
    projected = jnp.dot(inputs, weight_in, preferred_element_type=jnp.float32)
    gate_part = projected[:, :hidden_units]
    up_part = projected[:, hidden_units:]
    sigmoid_gate = jax.nn.sigmoid(gate_part)
    activated = gate_part * sigmoid_gate
    hidden = (activated * up_part).astype(jnp.bfloat16)
    backward = jnp.dot(upstream, weight_out.T, preferred_element_type=jnp.float32)
    prob_grad = jnp.sum(hidden.astype(jnp.float32) * backward, axis=1).astype(jnp.bfloat16)
    grad_gate = backward * up_part * sigmoid_gate * (1.0 + gate_part * (1.0 - sigmoid_gate))
    grad_up = backward * activated
    stacked = jnp.concatenate([grad_gate, grad_up], axis=1).astype(jnp.bfloat16)
    row_grads = jnp.dot(stacked, weight_in.T, preferred_element_type=jnp.float32).astype(
        jnp.bfloat16
    )
    return (row_grads, prob_grad)


def body(tokens, cotangent, gate_probs, experts, stratum, token_level, w_gate_up, w_down):
    axes = ("node", "local")
    device_count = lax.axis_size(axes)
    token_rows, chosen_count = experts.shape
    width = tokens.shape[1]
    capacity = max(2, token_rows * chosen_count * 5 // (4 * device_count))
    stratum_here = stratum[0]
    masked = token_level * STRATA < (stratum_here + 1) * LEVELS
    loss_weight = jnp.where(
        masked, STRATA / (stratum_here + 1).astype(jnp.float32), jnp.float32(0.0)
    )
    upstream = (cotangent.astype(jnp.float32) * loss_weight[:, None]).astype(jnp.bfloat16)
    chosen = experts.reshape(-1)
    pair_count = chosen.shape[0]
    onehot = (chosen[:, None] == jnp.arange(device_count, dtype=jnp.int32)[None, :]).astype(
        jnp.int32
    )
    ranking = jnp.sum((jnp.cumsum(onehot, axis=0) - 1) * onehot, axis=1)
    placed = chosen * capacity + ranking
    holder = placed[None, :] == jnp.arange(device_count * capacity, dtype=jnp.int32)[:, None]
    token_index = jnp.min(
        jnp.where(holder, jnp.arange(pair_count, dtype=jnp.int32)[None, :] // chosen_count, token_rows),
        axis=1,
    ).reshape(device_count, capacity)
    padded_tokens = jnp.concatenate([tokens, jnp.zeros((1, width), jnp.bfloat16)], axis=0)
    padded_upstream = jnp.concatenate([upstream, jnp.zeros((1, width), jnp.bfloat16)], axis=0)
    weight_in = w_gate_up[0]
    weight_out = w_down[0]
    sizes = CHUNK_SIZES if sum(CHUNK_SIZES) == capacity else (capacity,)
    starts = [sum(sizes[:c]) for c in range(len(sizes))]
    tiled = all((n * width) % (16 * 128) == 0 for n in sizes)
    rows = 16 if tiled else 1

    def block_of(n):
        return (device_count, rows, n * width // rows)

    def exchange(part):
        return lax.all_to_all(part, axes, 0, 0, tiled=True)

    sources = jnp.concatenate([padded_tokens, padded_upstream], axis=0)

    def send_of(c):
        index = token_index[:, starts[c] : starts[c] + sizes[c]]
        index = jnp.stack([index, index + (token_rows + 1)], axis=1).reshape(-1)
        return sources[index].reshape(device_count, 2 * rows, sizes[c] * width // rows)

    def compute(c, arrived):
        n = sizes[c]
        row_grads, prob_grad = expert_grads(
            arrived[:, :rows].reshape(device_count * n, width),
            arrived[:, rows:].reshape(device_count * n, width),
            weight_in,
            weight_out,
        )
        return row_grads.reshape(block_of(n)), prob_grad.reshape(device_count, n)

    def combine(c, home):
        n = sizes[c]
        local = ranking - starts[c]
        inside = (local >= 0) & (local < n)
        slot = jnp.where(inside, chosen * n + local, -1).reshape(token_rows, chosen_count)
        weight = jnp.where(inside.reshape(token_rows, chosen_count), gate_probs, 0.0)
        table = jnp.sum(
            jnp.where(
                slot[:, :, None] == jnp.arange(device_count * n, dtype=jnp.int32)[None, None, :],
                weight[:, :, None],
                0.0,
            ),
            axis=1,
        )
        high = table.astype(jnp.bfloat16)
        low = (table - high.astype(jnp.float32)).astype(jnp.bfloat16)
        home = home.reshape(device_count * n, width)
        return jnp.dot(high, home, preferred_element_type=jnp.float32) + jnp.dot(
            low, home, preferred_element_type=jnp.float32
        )

    last = len(sizes) - 1
    extra = rows * 128 if rows * 128 >= capacity else capacity
    extra_cols = extra // rows

    order = [((), (0,))]
    if last >= 1:
        order.append(((), (1,)))
    for c in range(2, len(sizes)):
        if sizes[c - 2] == sizes[c]:
            order.append(((c - 2,), (c,)))
        else:
            order += [((c - 2,), ()), ((), (c,))]
    for c in range(max(0, len(sizes) - 2), len(sizes)):
        order.append(((c,), ()))

    def final_block():
        probs = jnp.concatenate([prob_parts[i] for i in range(len(sizes))], axis=1)
        probs = jnp.pad(probs, ((0, 0), (0, extra - capacity))).reshape(
            device_count, rows, extra_cols
        )
        return jnp.concatenate([row_grads[last], probs], axis=2)

    arrived = {}
    returned = {}
    row_grads = {}
    prob_parts = {}

    def buffer_of(k):
        backs, sends = order[k]
        parts = [final_block() if n == last else row_grads[n] for n in backs]
        parts += [send_of(n) for n in sends]
        return parts[0] if len(parts) == 1 else jnp.concatenate(parts, axis=1)

    grad_tokens = None
    summed = set()
    buffer = buffer_of(0)
    for k, (backs, sends) in enumerate(order):
        done = exchange(buffer)
        computed = [n for n in (order[k + 1][0] if k + 1 < len(order) else ())]
        combined = []
        if not computed:
            combined = [n for n in sorted(returned) if n < last and n not in summed]
            summed.update(combined)
        for n in computed:
            row_grads[n], prob_parts[n] = compute(n, arrived[n])
        for n in combined:
            part = combine(n, returned[n])
            grad_tokens = part if grad_tokens is None else grad_tokens + part
        buffer = buffer_of(k + 1) if k + 1 < len(order) else None
        covered = (buffer, grad_tokens if combined else None)
        done, covered = lax.optimization_barrier((done, covered))
        buffer = covered[0]
        if combined:
            grad_tokens = covered[1]
        offset = 0
        for n in backs:
            returned[n] = done[:, offset : offset + rows] if len(backs) + len(sends) > 1 else done
            offset += rows
        for n in sends:
            arrived[n] = done[:, offset : offset + 2 * rows] if len(backs) + len(sends) > 1 else done
            offset += 2 * rows
    pending = returned[last]
    row_cols = sizes[last] * width // rows
    part = combine(last, pending[:, :, :row_cols])
    grad_tokens = part if grad_tokens is None else grad_tokens + part
    home_probs = pending[:, :, row_cols:].reshape(device_count, extra)[:, :capacity].reshape(-1)
    pick = placed[:, None] == jnp.arange(device_count * capacity, dtype=jnp.int32)[None, :]
    grad_probs = jnp.sum(
        jnp.where(pick, home_probs.astype(jnp.float32)[None, :], 0.0), axis=1
    ).astype(jnp.bfloat16)
    grad_probs = grad_probs.reshape(token_rows, chosen_count)
    return (grad_tokens.astype(jnp.bfloat16), grad_probs)


def solution(mesh):
    placed = (
        P(("node", "local"), None),
        P(("node", "local"), None),
        P(("node", "local"), None),
        P(("node", "local"), None),
        P(("node", "local")),
        P(("node", "local")),
        P(("node", "local"), None, None),
        P(("node", "local"), None, None),
    )
    return jax.shard_map(
        body,
        mesh=mesh,
        in_specs=placed,
        out_specs=(P(("node", "local"), None), P(("node", "local"), None)),
        check_vma=False,
    )
```

```python
import jax
import jax.numpy as jnp
from jax import lax
from jax.sharding import PartitionSpec as P

STRATA = 8
LEVELS = 64
CHUNK_SIZES = (3, 4, 3)


def expert_grads(inputs, upstream, weight_in, weight_out):
    hidden_units = weight_out.shape[0]
    projected = jnp.dot(inputs, weight_in, preferred_element_type=jnp.float32)
    gate_part = projected[:, :hidden_units]
    up_part = projected[:, hidden_units:]
    sigmoid_gate = jax.nn.sigmoid(gate_part)
    activated = gate_part * sigmoid_gate
    hidden = (activated * up_part).astype(jnp.bfloat16)
    backward = jnp.dot(upstream, weight_out.T, preferred_element_type=jnp.float32)
    prob_grad = jnp.sum(hidden.astype(jnp.float32) * backward, axis=1).astype(jnp.bfloat16)
    grad_gate = backward * up_part * sigmoid_gate * (1.0 + gate_part * (1.0 - sigmoid_gate))
    grad_up = backward * activated
    stacked = jnp.concatenate([grad_gate, grad_up], axis=1).astype(jnp.bfloat16)
    row_grads = jnp.dot(stacked, weight_in.T, preferred_element_type=jnp.float32).astype(
        jnp.bfloat16
    )
    return (row_grads, prob_grad)


def body(tokens, cotangent, gate_probs, experts, stratum, token_level, w_gate_up, w_down):
    axes = ("node", "local")
    device_count = lax.axis_size(axes)
    token_rows, chosen_count = experts.shape
    width = tokens.shape[1]
    capacity = max(2, token_rows * chosen_count * 5 // (4 * device_count))
    stratum_here = stratum[0]
    masked = token_level * STRATA < (stratum_here + 1) * LEVELS
    loss_weight = jnp.where(
        masked, STRATA / (stratum_here + 1).astype(jnp.float32), jnp.float32(0.0)
    )
    upstream = (cotangent.astype(jnp.float32) * loss_weight[:, None]).astype(jnp.bfloat16)
    chosen = experts.reshape(-1)
    pair_count = chosen.shape[0]
    onehot = (chosen[:, None] == jnp.arange(device_count, dtype=jnp.int32)[None, :]).astype(
        jnp.int32
    )
    ranking = jnp.sum((jnp.cumsum(onehot, axis=0) - 1) * onehot, axis=1)
    placed = chosen * capacity + ranking
    holder = placed[None, :] == jnp.arange(device_count * capacity, dtype=jnp.int32)[:, None]
    token_index = jnp.min(
        jnp.where(holder, jnp.arange(pair_count, dtype=jnp.int32)[None, :] // chosen_count, token_rows),
        axis=1,
    ).reshape(device_count, capacity)
    padded_tokens = jnp.concatenate([tokens, jnp.zeros((1, width), jnp.bfloat16)], axis=0)
    padded_upstream = jnp.concatenate([upstream, jnp.zeros((1, width), jnp.bfloat16)], axis=0)
    weight_in = w_gate_up[0]
    weight_out = w_down[0]
    sizes = CHUNK_SIZES if sum(CHUNK_SIZES) == capacity else (capacity,)
    starts = [sum(sizes[:c]) for c in range(len(sizes))]
    tiled = all((n * width) % (16 * 128) == 0 for n in sizes)
    rows = 16 if tiled else 1

    def block_of(n):
        return (device_count, rows, n * width // rows)

    def exchange(part):
        return lax.all_to_all(part, axes, 0, 0, tiled=True)

    sources = jnp.concatenate([padded_tokens, padded_upstream], axis=0)

    def send_of(c):
        index = token_index[:, starts[c] : starts[c] + sizes[c]]
        index = jnp.stack([index, index + (token_rows + 1)], axis=1).reshape(-1)
        pick = (index[:, None] == jnp.arange(sources.shape[0], dtype=jnp.int32)[None, :]).astype(
            jnp.bfloat16
        )
        picked = jnp.dot(pick, sources, preferred_element_type=jnp.float32).astype(jnp.bfloat16)
        return picked.reshape(device_count, 2 * rows, sizes[c] * width // rows)

    def compute(c, arrived):
        n = sizes[c]
        row_grads, prob_grad = expert_grads(
            arrived[:, :rows].reshape(device_count * n, width),
            arrived[:, rows:].reshape(device_count * n, width),
            weight_in,
            weight_out,
        )
        return row_grads.reshape(block_of(n)), prob_grad.reshape(device_count, n)

    def combine(c, home):
        n = sizes[c]
        local = ranking - starts[c]
        inside = (local >= 0) & (local < n)
        slot = jnp.where(inside, chosen * n + local, -1).reshape(token_rows, chosen_count)
        weight = jnp.where(inside.reshape(token_rows, chosen_count), gate_probs, 0.0)
        table = jnp.sum(
            jnp.where(
                slot[:, :, None] == jnp.arange(device_count * n, dtype=jnp.int32)[None, None, :],
                weight[:, :, None],
                0.0,
            ),
            axis=1,
        )
        high = table.astype(jnp.bfloat16)
        low = (table - high.astype(jnp.float32)).astype(jnp.bfloat16)
        home = home.reshape(device_count * n, width)
        return jnp.dot(high, home, preferred_element_type=jnp.float32) + jnp.dot(
            low, home, preferred_element_type=jnp.float32
        )

    last = len(sizes) - 1
    extra = rows * 128 if rows * 128 >= capacity else capacity
    extra_cols = extra // rows

    order = [((), (0,))]
    if last >= 1:
        order.append(((), (1,)))
    for c in range(2, len(sizes)):
        if sizes[c - 2] == sizes[c]:
            order.append(((c - 2,), (c,)))
        else:
            order += [((c - 2,), ()), ((), (c,))]
    for c in range(max(0, len(sizes) - 2), len(sizes)):
        order.append(((c,), ()))

    def final_block():
        probs = jnp.concatenate([prob_parts[i] for i in range(len(sizes))], axis=1)
        probs = jnp.pad(probs, ((0, 0), (0, extra - capacity))).reshape(
            device_count, rows, extra_cols
        )
        return jnp.concatenate([row_grads[last], probs], axis=2)

    arrived = {}
    returned = {}
    row_grads = {}
    prob_parts = {}

    def buffer_of(k):
        backs, sends = order[k]
        parts = [final_block() if n == last else row_grads[n] for n in backs]
        parts += [send_of(n) for n in sends]
        return parts[0] if len(parts) == 1 else jnp.concatenate(parts, axis=1)

    grad_tokens = None
    summed = set()
    buffer = buffer_of(0)
    for k, (backs, sends) in enumerate(order):
        done = exchange(buffer)
        computed = [n for n in (order[k + 1][0] if k + 1 < len(order) else ())]
        combined = []
        if not computed:
            combined = [n for n in sorted(returned) if n < last and n not in summed]
            summed.update(combined)
        for n in computed:
            row_grads[n], prob_parts[n] = compute(n, arrived[n])
        for n in combined:
            part = combine(n, returned[n])
            grad_tokens = part if grad_tokens is None else grad_tokens + part
        buffer = buffer_of(k + 1) if k + 1 < len(order) else None
        covered = (buffer, grad_tokens if combined else None)
        done, covered = lax.optimization_barrier((done, covered))
        buffer = covered[0]
        if combined:
            grad_tokens = covered[1]
        offset = 0
        for n in backs:
            returned[n] = done[:, offset : offset + rows] if len(backs) + len(sends) > 1 else done
            offset += rows
        for n in sends:
            arrived[n] = done[:, offset : offset + 2 * rows] if len(backs) + len(sends) > 1 else done
            offset += 2 * rows
    pending = returned[last]
    row_cols = sizes[last] * width // rows
    part = combine(last, pending[:, :, :row_cols])
    grad_tokens = part if grad_tokens is None else grad_tokens + part
    home_probs = pending[:, :, row_cols:].reshape(device_count, extra)[:, :capacity].reshape(-1)
    pick = placed[:, None] == jnp.arange(device_count * capacity, dtype=jnp.int32)[None, :]
    grad_probs = jnp.sum(
        jnp.where(pick, home_probs.astype(jnp.float32)[None, :], 0.0), axis=1
    ).astype(jnp.bfloat16)
    grad_probs = grad_probs.reshape(token_rows, chosen_count)
    return (grad_tokens.astype(jnp.bfloat16), grad_probs)


def solution(mesh):
    placed = (
        P(("node", "local"), None),
        P(("node", "local"), None),
        P(("node", "local"), None),
        P(("node", "local"), None),
        P(("node", "local")),
        P(("node", "local")),
        P(("node", "local"), None, None),
        P(("node", "local"), None, None),
    )
    return jax.shard_map(
        body,
        mesh=mesh,
        in_specs=placed,
        out_specs=(P(("node", "local"), None), P(("node", "local"), None)),
        check_vma=False,
    )
```

```python
import jax
import jax.numpy as jnp
from jax import lax
from jax.sharding import PartitionSpec as P

STRATA = 8
LEVELS = 64
CHUNK_SIZES = (3, 4, 3)


def expert_grads(inputs, upstream, weight_in, weight_out):
    hidden_units = weight_out.shape[0]
    projected = jnp.dot(inputs, weight_in, preferred_element_type=jnp.float32)
    gate_part = projected[:, :hidden_units]
    up_part = projected[:, hidden_units:]
    sigmoid_gate = jax.nn.sigmoid(gate_part)
    activated = gate_part * sigmoid_gate
    hidden = (activated * up_part).astype(jnp.bfloat16)
    backward = jnp.dot(upstream, weight_out.T, preferred_element_type=jnp.float32)
    prob_grad = jnp.sum(hidden.astype(jnp.float32) * backward, axis=1).astype(jnp.bfloat16)
    grad_gate = backward * up_part * sigmoid_gate * (1.0 + gate_part * (1.0 - sigmoid_gate))
    grad_up = backward * activated
    stacked = jnp.concatenate([grad_gate, grad_up], axis=1).astype(jnp.bfloat16)
    row_grads = jnp.dot(stacked, weight_in.T, preferred_element_type=jnp.float32).astype(
        jnp.bfloat16
    )
    return (row_grads, prob_grad)


def body(tokens, cotangent, gate_probs, experts, stratum, token_level, w_gate_up, w_down):
    axes = ("node", "local")
    device_count = lax.axis_size(axes)
    token_rows, chosen_count = experts.shape
    width = tokens.shape[1]
    capacity = max(2, token_rows * chosen_count * 5 // (4 * device_count))
    stratum_here = stratum[0]
    masked = token_level * STRATA < (stratum_here + 1) * LEVELS
    loss_weight = jnp.where(
        masked, STRATA / (stratum_here + 1).astype(jnp.float32), jnp.float32(0.0)
    )
    upstream = (cotangent.astype(jnp.float32) * loss_weight[:, None]).astype(jnp.bfloat16)
    chosen = experts.reshape(-1)
    pair_count = chosen.shape[0]
    order_of = jnp.arange(pair_count, dtype=jnp.int32)
    earlier = (chosen[None, :] == chosen[:, None]) & (order_of[None, :] < order_of[:, None])
    ranking = jnp.sum(earlier.astype(jnp.int32), axis=1)
    placed = chosen * capacity + ranking
    holder = placed[None, :] == jnp.arange(device_count * capacity, dtype=jnp.int32)[:, None]
    token_index = jnp.min(
        jnp.where(holder, jnp.arange(pair_count, dtype=jnp.int32)[None, :] // chosen_count, token_rows),
        axis=1,
    ).reshape(device_count, capacity)
    padded_tokens = jnp.concatenate([tokens, jnp.zeros((1, width), jnp.bfloat16)], axis=0)
    padded_upstream = jnp.concatenate([upstream, jnp.zeros((1, width), jnp.bfloat16)], axis=0)
    weight_in = w_gate_up[0]
    weight_out = w_down[0]
    sizes = CHUNK_SIZES if sum(CHUNK_SIZES) == capacity else (capacity,)
    starts = [sum(sizes[:c]) for c in range(len(sizes))]
    tiled = all((n * width) % (16 * 128) == 0 for n in sizes)
    rows = 16 if tiled else 1

    def block_of(n):
        return (device_count, rows, n * width // rows)

    def exchange(part):
        return lax.all_to_all(part, axes, 0, 0, tiled=True)

    sources = jnp.concatenate([padded_tokens, padded_upstream], axis=0)

    def send_of(c):
        index = token_index[:, starts[c] : starts[c] + sizes[c]]
        index = jnp.stack([index, index + (token_rows + 1)], axis=1).reshape(-1)
        return sources[index].reshape(device_count, 2 * rows, sizes[c] * width // rows)

    def compute(c, arrived):
        n = sizes[c]
        row_grads, prob_grad = expert_grads(
            arrived[:, :rows].reshape(device_count * n, width),
            arrived[:, rows:].reshape(device_count * n, width),
            weight_in,
            weight_out,
        )
        return row_grads.reshape(block_of(n)), prob_grad.reshape(device_count, n)

    def combine(c, home):
        n = sizes[c]
        local = ranking - starts[c]
        inside = (local >= 0) & (local < n)
        slot = jnp.where(inside, chosen * n + local, -1).reshape(token_rows, chosen_count)
        weight = jnp.where(inside.reshape(token_rows, chosen_count), gate_probs, 0.0)
        table = jnp.sum(
            jnp.where(
                slot[:, :, None] == jnp.arange(device_count * n, dtype=jnp.int32)[None, None, :],
                weight[:, :, None],
                0.0,
            ),
            axis=1,
        )
        high = table.astype(jnp.bfloat16)
        low = (table - high.astype(jnp.float32)).astype(jnp.bfloat16)
        home = home.reshape(device_count * n, width)
        return jnp.dot(high, home, preferred_element_type=jnp.float32) + jnp.dot(
            low, home, preferred_element_type=jnp.float32
        )

    last = len(sizes) - 1
    extra = rows * 128 if rows * 128 >= capacity else capacity
    extra_cols = extra // rows

    order = [((), (0,))]
    if last >= 1:
        order.append(((), (1,)))
    for c in range(2, len(sizes)):
        if sizes[c - 2] == sizes[c]:
            order.append(((c - 2,), (c,)))
        else:
            order += [((c - 2,), ()), ((), (c,))]
    for c in range(max(0, len(sizes) - 2), len(sizes)):
        order.append(((c,), ()))

    def final_block():
        probs = jnp.concatenate([prob_parts[i] for i in range(len(sizes))], axis=1)
        probs = jnp.pad(probs, ((0, 0), (0, extra - capacity))).reshape(
            device_count, rows, extra_cols
        )
        return jnp.concatenate([row_grads[last], probs], axis=2)

    arrived = {}
    returned = {}
    row_grads = {}
    prob_parts = {}

    def buffer_of(k):
        backs, sends = order[k]
        parts = [final_block() if n == last else row_grads[n] for n in backs]
        parts += [send_of(n) for n in sends]
        return parts[0] if len(parts) == 1 else jnp.concatenate(parts, axis=1)

    grad_tokens = None
    summed = set()
    buffer = buffer_of(0)
    for k, (backs, sends) in enumerate(order):
        done = exchange(buffer)
        computed = [n for n in (order[k + 1][0] if k + 1 < len(order) else ())]
        combined = []
        if not computed:
            combined = [n for n in sorted(returned) if n < last and n not in summed]
            summed.update(combined)
        for n in computed:
            row_grads[n], prob_parts[n] = compute(n, arrived[n])
        for n in combined:
            part = combine(n, returned[n])
            grad_tokens = part if grad_tokens is None else grad_tokens + part
        buffer = buffer_of(k + 1) if k + 1 < len(order) else None
        covered = (buffer, grad_tokens if combined else None)
        done, covered = lax.optimization_barrier((done, covered))
        buffer = covered[0]
        if combined:
            grad_tokens = covered[1]
        offset = 0
        for n in backs:
            returned[n] = done[:, offset : offset + rows] if len(backs) + len(sends) > 1 else done
            offset += rows
        for n in sends:
            arrived[n] = done[:, offset : offset + 2 * rows] if len(backs) + len(sends) > 1 else done
            offset += 2 * rows
    pending = returned[last]
    row_cols = sizes[last] * width // rows
    part = combine(last, pending[:, :, :row_cols])
    grad_tokens = part if grad_tokens is None else grad_tokens + part
    home_probs = pending[:, :, row_cols:].reshape(device_count, extra)[:, :capacity].reshape(-1)
    pick = placed[:, None] == jnp.arange(device_count * capacity, dtype=jnp.int32)[None, :]
    grad_probs = jnp.sum(
        jnp.where(pick, home_probs.astype(jnp.float32)[None, :], 0.0), axis=1
    ).astype(jnp.bfloat16)
    grad_probs = grad_probs.reshape(token_rows, chosen_count)
    return (grad_tokens.astype(jnp.bfloat16), grad_probs)


def solution(mesh):
    placed = (
        P(("node", "local"), None),
        P(("node", "local"), None),
        P(("node", "local"), None),
        P(("node", "local"), None),
        P(("node", "local")),
        P(("node", "local")),
        P(("node", "local"), None, None),
        P(("node", "local"), None, None),
    )
    return jax.shard_map(
        body,
        mesh=mesh,
        in_specs=placed,
        out_specs=(P(("node", "local"), None), P(("node", "local"), None)),
        check_vma=False,
    )
```

```python
import jax
import jax.numpy as jnp
from jax import lax
from jax.sharding import PartitionSpec as P

STRATA = 8
LEVELS = 64
CHUNK_SIZES = (3, 4, 3)


def expert_grads(inputs, upstream, weight_in, weight_out):
    hidden_units = weight_out.shape[0]
    projected = jnp.dot(inputs, weight_in, preferred_element_type=jnp.float32)
    gate_part = projected[:, :hidden_units]
    up_part = projected[:, hidden_units:]
    sigmoid_gate = jax.nn.sigmoid(gate_part)
    activated = gate_part * sigmoid_gate
    hidden = (activated * up_part).astype(jnp.bfloat16)
    backward = jnp.dot(upstream, weight_out.T, preferred_element_type=jnp.float32)
    prob_grad = jnp.sum(hidden.astype(jnp.float32) * backward, axis=1).astype(jnp.bfloat16)
    grad_gate = backward * up_part * sigmoid_gate * (1.0 + gate_part * (1.0 - sigmoid_gate))
    grad_up = backward * activated
    stacked = jnp.concatenate([grad_gate, grad_up], axis=1).astype(jnp.bfloat16)
    row_grads = jnp.dot(stacked, weight_in.T, preferred_element_type=jnp.float32).astype(
        jnp.bfloat16
    )
    return (row_grads, prob_grad)


def body(tokens, cotangent, gate_probs, experts, stratum, token_level, w_gate_up, w_down):
    axes = ("node", "local")
    device_count = lax.axis_size(axes)
    token_rows, chosen_count = experts.shape
    width = tokens.shape[1]
    capacity = max(2, token_rows * chosen_count * 5 // (4 * device_count))
    stratum_here = stratum[0]
    masked = token_level * STRATA < (stratum_here + 1) * LEVELS
    loss_weight = jnp.where(
        masked, STRATA / (stratum_here + 1).astype(jnp.float32), jnp.float32(0.0)
    )
    upstream = (cotangent.astype(jnp.float32) * loss_weight[:, None]).astype(jnp.bfloat16)
    chosen = experts.reshape(-1)
    pair_count = chosen.shape[0]
    onehot = (chosen[:, None] == jnp.arange(device_count, dtype=jnp.int32)[None, :]).astype(
        jnp.int32
    )
    ranking = jnp.sum((jnp.cumsum(onehot, axis=0) - 1) * onehot, axis=1)
    placed = chosen * capacity + ranking
    holder = placed[None, :] == jnp.arange(device_count * capacity, dtype=jnp.int32)[:, None]
    token_index = jnp.min(
        jnp.where(holder, jnp.arange(pair_count, dtype=jnp.int32)[None, :] // chosen_count, token_rows),
        axis=1,
    ).reshape(device_count, capacity)
    padded_tokens = jnp.concatenate([tokens, jnp.zeros((1, width), jnp.bfloat16)], axis=0)
    padded_upstream = jnp.concatenate([upstream, jnp.zeros((1, width), jnp.bfloat16)], axis=0)
    weight_in = w_gate_up[0]
    weight_out = w_down[0]
    sizes = CHUNK_SIZES if sum(CHUNK_SIZES) == capacity else (capacity,)
    starts = [sum(sizes[:c]) for c in range(len(sizes))]
    cols = 256 if all((n * width) % (16 * 256) == 0 for n in sizes) else width

    def rows_of(n):
        return n * width // cols

    def block_of(n):
        return (device_count, rows_of(n), cols)

    def exchange(part):
        return lax.all_to_all(part, axes, 0, 0, tiled=True)

    sources = jnp.concatenate([padded_tokens, padded_upstream], axis=0)

    def send_of(c):
        index = token_index[:, starts[c] : starts[c] + sizes[c]]
        index = jnp.stack([index, index + (token_rows + 1)], axis=1).reshape(-1)
        return sources[index].reshape(device_count, 2 * rows_of(sizes[c]), cols)

    def compute(c, arrived):
        n = sizes[c]
        row_grads, prob_grad = expert_grads(
            arrived[:, : rows_of(n)].reshape(device_count * n, width),
            arrived[:, rows_of(n) :].reshape(device_count * n, width),
            weight_in,
            weight_out,
        )
        return row_grads.reshape(block_of(n)), prob_grad.reshape(device_count, n)

    def combine(c, home):
        n = sizes[c]
        local = ranking - starts[c]
        inside = (local >= 0) & (local < n)
        slot = jnp.where(inside, chosen * n + local, -1).reshape(token_rows, chosen_count)
        weight = jnp.where(inside.reshape(token_rows, chosen_count), gate_probs, 0.0)
        table = jnp.sum(
            jnp.where(
                slot[:, :, None] == jnp.arange(device_count * n, dtype=jnp.int32)[None, None, :],
                weight[:, :, None],
                0.0,
            ),
            axis=1,
        )
        high = table.astype(jnp.bfloat16)
        low = (table - high.astype(jnp.float32)).astype(jnp.bfloat16)
        home = home.reshape(device_count * n, width)
        return jnp.dot(high, home, preferred_element_type=jnp.float32) + jnp.dot(
            low, home, preferred_element_type=jnp.float32
        )

    last = len(sizes) - 1
    extra_rows = 16 if 16 * cols >= capacity else -(-capacity // cols)
    extra = extra_rows * cols

    order = [((), (0,))]
    if last >= 1:
        order.append(((), (1,)))
    for c in range(2, len(sizes)):
        if sizes[c - 2] == sizes[c]:
            order.append(((c - 2,), (c,)))
        else:
            order += [((c - 2,), ()), ((), (c,))]
    for c in range(max(0, len(sizes) - 2), len(sizes)):
        order.append(((c,), ()))

    def final_block():
        probs = jnp.concatenate([prob_parts[i] for i in range(len(sizes))], axis=1)
        probs = jnp.pad(probs, ((0, 0), (0, extra - capacity))).reshape(
            device_count, extra_rows, cols
        )
        return jnp.concatenate([row_grads[last], probs], axis=1)

    arrived = {}
    returned = {}
    row_grads = {}
    prob_parts = {}

    def buffer_of(k):
        backs, sends = order[k]
        parts = [final_block() if n == last else row_grads[n] for n in backs]
        parts += [send_of(n) for n in sends]
        return parts[0] if len(parts) == 1 else jnp.concatenate(parts, axis=1)

    grad_tokens = None
    summed = set()
    buffer = buffer_of(0)
    for k, (backs, sends) in enumerate(order):
        done = exchange(buffer)
        computed = [n for n in (order[k + 1][0] if k + 1 < len(order) else ())]
        combined = []
        if not computed:
            combined = [n for n in sorted(returned) if n < last and n not in summed]
            summed.update(combined)
        for n in computed:
            row_grads[n], prob_parts[n] = compute(n, arrived[n])
        for n in combined:
            part = combine(n, returned[n])
            grad_tokens = part if grad_tokens is None else grad_tokens + part
        buffer = buffer_of(k + 1) if k + 1 < len(order) else None
        covered = (buffer, grad_tokens if combined else None)
        done, covered = lax.optimization_barrier((done, covered))
        buffer = covered[0]
        if combined:
            grad_tokens = covered[1]
        offset = 0
        for n in backs:
            height = rows_of(sizes[n]) + (extra_rows if n == last else 0)
            returned[n] = done[:, offset : offset + height] if len(backs) + len(sends) > 1 else done
            offset += height
        for n in sends:
            arrived[n] = done[:, offset : offset + 2 * rows_of(sizes[n])] if len(backs) + len(sends) > 1 else done
            offset += 2 * rows_of(sizes[n])
    pending = returned[last]
    row_count = rows_of(sizes[last])
    part = combine(last, pending[:, :row_count])
    grad_tokens = part if grad_tokens is None else grad_tokens + part
    home_probs = pending[:, row_count:].reshape(device_count, extra)[:, :capacity].reshape(-1)
    pick = placed[:, None] == jnp.arange(device_count * capacity, dtype=jnp.int32)[None, :]
    grad_probs = jnp.sum(
        jnp.where(pick, home_probs.astype(jnp.float32)[None, :], 0.0), axis=1
    ).astype(jnp.bfloat16)
    grad_probs = grad_probs.reshape(token_rows, chosen_count)
    return (grad_tokens.astype(jnp.bfloat16), grad_probs)


def solution(mesh):
    placed = (
        P(("node", "local"), None),
        P(("node", "local"), None),
        P(("node", "local"), None),
        P(("node", "local"), None),
        P(("node", "local")),
        P(("node", "local")),
        P(("node", "local"), None, None),
        P(("node", "local"), None, None),
    )
    return jax.shard_map(
        body,
        mesh=mesh,
        in_specs=placed,
        out_specs=(P(("node", "local"), None), P(("node", "local"), None)),
        check_vma=False,
    )
```
